32 devices in a mesh: bucket: 8 (over z, x), rel: 4 (over y, core).
Axes of the slice: x: 2, y: 2, z: 4, core: 2. Of those that a mesh axis runs over, the one named last changes fastest.
Arguments:
- left_rows: float32 [8192, 512], P(('bucket', 'rel')), may hold values from -1.2 to 1.2
- left_state: float32 [8192], P(('bucket', 'rel')), may hold values from 1e-06 to 0.0001
- right_rows: float32 [8192, 512], P(('bucket', 'rel')), may hold values from -1.2 to 1.2
- right_state: float32 [8192], P(('bucket', 'rel')), may hold values from 1e-06 to 0.0001
- relations: bfloat16 [4, 512, 512], P('rel'), may hold values from -0.25 to 0.25
- fetch_ids: int32 [8, 4, 4], P('bucket', 'rel'), may hold values from 0 to 3
- edge_left: int32 [8, 4, 2, 512], P('bucket', 'rel'), may hold values from 0 to 255
- edge_right: int32 [8, 4, 2, 512], P('bucket', 'rel'), may hold values from 0 to 255
- edge_slot: int32 [8, 4, 2, 512], P('bucket', 'rel'), may hold values from 0 to 1
- edge_weight: int32 [8, 4, 2, 512], P('bucket', 'rel'), may hold values from 1 to 4
- matching: int32 [1], replicated, may hold values from 1 to 7
Outputs:
- left_out: float32 [8192, 512], P(('bucket', 'rel'))
- left_state_out: float32 [8192], P(('bucket', 'rel'))
- right_out: float32 [8192, 512], P(('bucket', 'rel'))
- right_state_out: float32 [8192], P(('bucket', 'rel'))
- rel_grad: float32 [4, 512, 512], P('rel')
The draws below stay inside these ranges and needn't reach their ends.
Inputs may be any that keep to these rules, and one draw needn't show every extreme that they name: Bucket b is paired with bucket b XOR matching.
All inputs are finite; a program needn't handle non-finite values.
Results may differ from the reference program's by a relative error of at most 0.0015.
The reference program's roundings to bfloat16 on the way count: a program that leaves them out, or rounds other values in their place, can miss the bound.
Values may be sent and summed in bfloat16 or wider, within the bound.
No kernel may reach another device: no remote copies, remote signals or barrier semaphores. Data moves between devices by JAX's collectives and lax.ppermute only.
A program may use at most 64 MiB of HBM per device.

```python
import math
import jax
import jax.numpy as jnp
import numpy as np
from jax import lax

D = 512
E_DEV = 256
NREL = 4
EDGES = 512
ROWS = 8192
N_BUCKET = 8
N_REL = 4


def with_ends(result, stream_key, least, largest):
    spot = [jax.random.randint(jax.random.fold_in(stream_key, axis), (), 0, length) for axis, length in enumerate(result.shape)]
    main_axis = result.shape.index(max(result.shape))
    next_to = spot[:main_axis] + [(spot[main_axis] + 1) % result.shape[main_axis]] + spot[main_axis + 1:]
    return result.at[tuple(spot)].set(least).at[tuple(next_to)].set(largest)


def steps_of(rng, shape, cuts, low, high):
    level = 1.0
    for dim, blocks in cuts:
        draws = jax.random.uniform(jax.random.fold_in(jax.random.fold_in(rng, 6), dim), (blocks,), jnp.float32, low / len(cuts), high / len(cuts))
        level = level * jnp.repeat(jnp.exp(draws), shape[dim] // blocks).reshape((-1,) + (1,) * (len(shape) - 1 - dim))
    return level


def rank_table(number_of, skew):
    loads = [(1 << 20) // math.isqrt(rank ** skew) + 1 for rank in range(1, number_of + 1)]
    scale = 1 + sum(loads) // (1 << 30)
    return np.cumsum(np.array([max(1, weight // scale) for weight in loads]))


def ranked_ids(stream_key, extent, number_of, skew):
    listing = rank_table(number_of, skew)
    ticket = jax.random.randint(jax.random.fold_in(stream_key, 1), extent, 0, int(listing[number_of - 1]))
    rank = jnp.searchsorted(jnp.asarray(listing, jnp.int32), ticket, side="right")
    return jax.random.permutation(jax.random.fold_in(stream_key, 2), number_of)[rank].astype(jnp.int32)


def gaussian(own_key, shape, spread, most, cuts=(), kind=jnp.bfloat16):
    values = spread * jax.random.normal(own_key, shape, jnp.float32)
    if cuts:
        values = values * steps_of(own_key, shape, cuts, -0.22, 0.18)
    return jnp.clip(values, -most, most).astype(kind)


def setup_inputs(seed: int = 0) -> dict:
    splits = jax.random.split(jax.random.key(seed), 12)
    return {
        "left_rows": gaussian(splits[0], (ROWS, D), 0.2, 1.2, ((0, 32),), jnp.float32),
        "left_state": jnp.clip(jnp.exp(math.log(0.0001) - 4.6051702 * jax.random.uniform(splits[1], (ROWS,), jnp.float32) ** steps_of(splits[1], (ROWS,), ((0, 32),), -0.2, 0.2)), 9.999999974752427e-07, 0.0001),
        "right_rows": gaussian(splits[2], (ROWS, D), 0.2, 1.2, ((0, 32),), jnp.float32),
        "right_state": jnp.clip(jnp.exp(math.log(0.0001) - 4.6051702 * jax.random.uniform(splits[3], (ROWS,), jnp.float32) ** steps_of(splits[3], (ROWS,), ((0, 32),), -0.2, 0.2)), 9.999999974752427e-07, 0.0001),
        "relations": gaussian(splits[4], (NREL, D, D), D ** -0.5, 0.25, ((0, 4),)),
        "fetch_ids": with_ends(ranked_ids(splits[5], (N_BUCKET, N_REL, 4), NREL, 2), jax.random.fold_in(splits[5], 3), 0, NREL - 1).astype(jnp.int32),
        "edge_left": with_ends(jax.random.randint(splits[6], (N_BUCKET, N_REL, 2, EDGES), 0, E_DEV), jax.random.fold_in(splits[6], 1), 0, E_DEV - 1).astype(jnp.int32),
        "edge_right": with_ends(jax.random.randint(splits[7], (N_BUCKET, N_REL, 2, EDGES), 0, E_DEV), jax.random.fold_in(splits[7], 1), 0, E_DEV - 1).astype(jnp.int32),
        "edge_slot": with_ends(jax.random.randint(splits[8], (N_BUCKET, N_REL, 2, EDGES), 0, 2), jax.random.fold_in(splits[8], 1), 0, 1).astype(jnp.int32),
        "edge_weight": with_ends(jax.random.randint(splits[9], (N_BUCKET, N_REL, 2, EDGES), 1, 5), jax.random.fold_in(splits[9], 1), 1, 4).astype(jnp.int32),
        "matching": jax.random.randint(splits[10], (1,), 1, N_BUCKET).astype(jnp.int32),
    }


learn_rate = 0.1

def edge_targets(edge_left, edge_right, edge_slot, edge_weight, block_len):
    table = jnp.zeros((2, block_len, block_len), jnp.float32)
    table = table.at[edge_slot, edge_left, edge_right].add(edge_weight.astype(jnp.float32))
    return [table[0], table[1]]

def adagrad(table, state, gradient):
    state_new = state + lax.optimization_barrier(jnp.mean(gradient * gradient, axis=1))
    return (table - learn_rate * gradient / jnp.sqrt(state_new)[:, None], state_new)

def one_round(left_block, left_st, right_block, right_st, rel_pair, edge_left, edge_right, edge_slot, edge_weight):
    block_len = left_block.shape[0]
    left_half = left_block.astype(jnp.bfloat16)
    right_half = right_block.astype(jnp.bfloat16)
    targets = edge_targets(edge_left, edge_right, edge_slot, edge_weight, block_len)
    grad_left = jnp.zeros(left_block.shape, jnp.float32)
    grad_right = jnp.zeros(right_block.shape, jnp.float32)
    rel_grads = []
    for slot_index in range(2):
        matrix = rel_pair[slot_index]
        projected = jnp.dot(left_half, matrix, preferred_element_type=jnp.float32).astype(jnp.bfloat16)
        scores = jnp.dot(projected, right_half.T, preferred_element_type=jnp.float32)
        score_grad = ((jax.nn.sigmoid(scores) - targets[slot_index]) / block_len).astype(jnp.bfloat16)
        carried = jnp.dot(score_grad, right_half, preferred_element_type=jnp.float32).astype(jnp.bfloat16)
        grad_left = grad_left + jnp.dot(carried, matrix.T, preferred_element_type=jnp.float32)
        grad_right = grad_right + jnp.dot(score_grad.T, projected, preferred_element_type=jnp.float32)
        rel_grads.append(jnp.dot(left_half.T, carried, preferred_element_type=jnp.float32))
    left_new, left_st_new = adagrad(left_block, left_st, grad_left)
    right_new, right_st_new = adagrad(right_block, right_st, grad_right)
    return (left_new, left_st_new, right_new, right_st_new, rel_grads)

def reference(left_rows, left_state, right_rows, right_state, relations, fetch_ids, edge_left, edge_right, edge_slot, edge_weight, matching):
    devices_all = N_BUCKET * N_REL
    left_blocks = left_rows.reshape(devices_all, E_DEV, D)
    left_states = left_state.reshape(devices_all, E_DEV)
    right_blocks = right_rows.reshape(devices_all, E_DEV, D)
    right_states = right_state.reshape(devices_all, E_DEV)
    fetch_flat = fetch_ids.reshape(devices_all, 4)
    lefts = edge_left.reshape(devices_all, 2, EDGES)
    rights = edge_right.reshape(devices_all, 2, EDGES)
    slots = edge_slot.reshape(devices_all, 2, EDGES)
    weights = edge_weight.reshape(devices_all, 2, EDGES)
    partner = jnp.bitwise_xor(jnp.arange(N_BUCKET, dtype=jnp.int32), matching[0])
    accum = jnp.zeros((NREL, D, D), jnp.float32)
    for round_index in range(2):

        def visit_device(summed, inputs):
            left_block, left_st, right_block, right_st, rel_ids, e_left, e_right, e_slot, e_weight = inputs
            chosen = rel_ids[2 * round_index:2 * round_index + 2]
            rel_pair = jnp.take(relations, chosen, axis=0)
            left_new, left_st_new, right_new, right_st_new, rel_grads = one_round(left_block, left_st, right_block, right_st, rel_pair, e_left[round_index], e_right[round_index], e_slot[round_index], e_weight[round_index])
            summed = summed.at[chosen[0]].add(rel_grads[0])
            summed = summed.at[chosen[1]].add(rel_grads[1])
            return (summed, (left_new, left_st_new, right_new, right_st_new))
        accum, results = lax.scan(visit_device, accum, (left_blocks, left_states, right_blocks, right_states, fetch_flat, lefts, rights, slots, weights))
        left_blocks, left_states, right_blocks, right_states = results
        if round_index == 0:
            right_blocks = right_blocks.reshape(N_BUCKET, N_REL, E_DEV, D)[partner].reshape(devices_all, E_DEV, D)
            right_states = right_states.reshape(N_BUCKET, N_REL, E_DEV)[partner].reshape(devices_all, E_DEV)
    return (left_blocks.reshape(ROWS, D), left_states.reshape(ROWS), right_blocks.reshape(ROWS, D), right_states.reshape(ROWS), accum)
```

```python
import jax
import jax.numpy as jnp
from jax import lax
from jax.sharding import PartitionSpec as P

learn_rate = 0.1


def edge_targets(edge_left, edge_right, edge_slot, edge_weight, block_len):
    rows = jnp.arange(block_len, dtype=jnp.int32)
    weight = edge_weight.astype(jnp.float32)
    right_hot = (edge_right[:, None] == rows[None, :]).astype(jnp.bfloat16)
    left_hot = edge_left[:, None] == rows[None, :]
    targets = []
    for slot_index in range(2):
        scale = jnp.where(edge_slot == slot_index, weight, jnp.float32(0.0))
        left_w = jnp.where(left_hot, scale[:, None], jnp.float32(0.0)).astype(jnp.bfloat16)
        targets.append(
            lax.dot_general(
                left_w, right_hot, (((0,), (0,)), ((), ())), preferred_element_type=jnp.float32
            )
        )
    return targets


def adagrad(table, state, gradient):
    state_new = state + jnp.mean(gradient * gradient, axis=1)
    return (table - learn_rate * gradient / jnp.sqrt(state_new)[:, None], state_new)


def one_round(
    left_block,
    left_st,
    right_block,
    right_st,
    rel_pair,
    edge_left,
    edge_right,
    edge_slot,
    edge_weight,
):
    block_len = left_block.shape[0]
    left_half = left_block.astype(jnp.bfloat16)
    right_half = right_block.astype(jnp.bfloat16)
    targets = edge_targets(edge_left, edge_right, edge_slot, edge_weight, block_len)
    grad_left = jnp.zeros(left_block.shape, jnp.float32)
    grad_right = jnp.zeros(right_block.shape, jnp.float32)
    rel_grads = []
    for slot_index in range(2):
        matrix = rel_pair[slot_index]
        projected = jnp.dot(left_half, matrix, preferred_element_type=jnp.float32).astype(
            jnp.bfloat16
        )
        scores = jnp.dot(projected, right_half.T, preferred_element_type=jnp.float32)
        score_grad = ((jax.nn.sigmoid(scores) - targets[slot_index]) / block_len).astype(
            jnp.bfloat16
        )
        carried = jnp.dot(score_grad, right_half, preferred_element_type=jnp.float32).astype(
            jnp.bfloat16
        )
        grad_left = grad_left + jnp.dot(carried, matrix.T, preferred_element_type=jnp.float32)
        grad_right = grad_right + jnp.dot(
            score_grad.T, projected, preferred_element_type=jnp.float32
        )
        rel_grads.append(jnp.dot(left_half.T, carried, preferred_element_type=jnp.float32))
    left_new, left_st_new = adagrad(left_block, left_st, grad_left)
    right_new, right_st_new = adagrad(right_block, right_st, grad_right)
    return (left_new, left_st_new, right_new, right_st_new, rel_grads)


def partner_blocks(row_block, state_block, switch):
    count = lax.axis_size("bucket")

    def exchange(offset):
        pairs = [(b, b ^ offset) for b in range(count)]

        def run(rows, states):
            return (lax.ppermute(rows, "bucket", pairs), lax.ppermute(states, "bucket", pairs))

        return run

    branches = [exchange(offset) for offset in range(1, count)]
    return lax.switch(switch - 1, branches, row_block, state_block)


def reduce_gradients(gradients, rel_ids, rel_total, width):
    stacked = jnp.stack(gradients)
    own_rows = rel_total // lax.axis_size("rel") * width
    rel_count_piece = own_rows * lax.axis_size("rel") // width
    rel_list = jnp.arange(rel_count_piece, dtype=jnp.int32)
    weights = (rel_ids[:, None] == rel_list[None, :]).astype(jnp.float32)
    term = jnp.einsum("sk,sde->kde", weights, stacked, precision=lax.Precision.HIGHEST)
    partial_sum = lax.psum_scatter(
        term.reshape(rel_count_piece * width, width), "rel", scatter_dimension=0, tiled=True
    )
    return lax.psum(partial_sum, "bucket")


def on_device(
    left_rows,
    left_state,
    right_rows,
    right_state,
    relations,
    fetch_ids,
    edge_left,
    edge_right,
    edge_slot,
    edge_weight,
    matching,
):
    width = relations.shape[1]
    rel_table = lax.all_gather(relations, "rel", axis=0, tiled=True)
    rel_total = rel_table.shape[0]
    rel_ids = fetch_ids[0, 0]
    switch = matching[0]
    table_left, state_left = (left_rows, left_state)
    row_block, state_block = (right_rows, right_state)
    gradients = []
    for round_index in range(2):
        rel_pair = jnp.take(rel_table, rel_ids[2 * round_index : 2 * round_index + 2], axis=0)
        table_left, state_left, row_block, state_block, rel_grads = one_round(
            table_left,
            state_left,
            row_block,
            state_block,
            rel_pair,
            edge_left[0, 0, round_index],
            edge_right[0, 0, round_index],
            edge_slot[0, 0, round_index],
            edge_weight[0, 0, round_index],
        )
        gradients.extend(rel_grads)
        if round_index == 0:
            row_block, state_block = partner_blocks(row_block, state_block, switch)
    owned = reduce_gradients(gradients, rel_ids, rel_total, width)
    return (table_left, state_left, row_block, state_block, owned.reshape(-1, width, width))


def solution(mesh):
    in_specs = (
        P(("bucket", "rel"), None),
        P(("bucket", "rel")),
        P(("bucket", "rel"), None),
        P(("bucket", "rel")),
        P("rel", None, None),
        P("bucket", "rel", None),
        P("bucket", "rel", None, None),
        P("bucket", "rel", None, None),
        P("bucket", "rel", None, None),
        P("bucket", "rel", None, None),
        P(),
    )
    out_specs = (
        P(("bucket", "rel"), None),
        P(("bucket", "rel")),
        P(("bucket", "rel"), None),
        P(("bucket", "rel")),
        P("rel", None, None),
    )
    return jax.shard_map(
        on_device, mesh=mesh, in_specs=in_specs, out_specs=out_specs, check_vma=False
    )
```

```python
import jax
import jax.numpy as jnp
from jax import lax
from jax.sharding import PartitionSpec as P

learn_rate = 0.1


def edge_targets(edge_left, edge_right, edge_slot, edge_weight, block_len):
    rows = jnp.arange(block_len, dtype=jnp.int32)
    weight = edge_weight.astype(jnp.float32)
    right_hot = (edge_right[:, None] == rows[None, :]).astype(jnp.bfloat16)
    left_hot = edge_left[:, None] == rows[None, :]
    targets = []
    for slot_index in range(2):
        scale = jnp.where(edge_slot == slot_index, weight, jnp.float32(0.0))
        left_w = jnp.where(left_hot, scale[:, None], jnp.float32(0.0)).astype(jnp.bfloat16)
        targets.append(
            lax.dot_general(
                left_w, right_hot, (((0,), (0,)), ((), ())), preferred_element_type=jnp.float32
            )
        )
    return targets


def adagrad(table, state, gradient):
    state_new = state + jnp.mean(gradient * gradient, axis=1)
    return (table - learn_rate * gradient / jnp.sqrt(state_new)[:, None], state_new)


def one_round(
    left_block,
    left_st,
    right_block,
    right_st,
    rel_pair,
    edge_left,
    edge_right,
    edge_slot,
    edge_weight,
):
    block_len = left_block.shape[0]
    left_half = left_block.astype(jnp.bfloat16)
    right_half = right_block.astype(jnp.bfloat16)
    targets = edge_targets(edge_left, edge_right, edge_slot, edge_weight, block_len)
    grad_left = jnp.zeros(left_block.shape, jnp.float32)
    grad_right = jnp.zeros(right_block.shape, jnp.float32)
    rel_grads = []
    for slot_index in range(2):
        matrix = rel_pair[slot_index]
        projected = jnp.dot(left_half, matrix, preferred_element_type=jnp.float32).astype(
            jnp.bfloat16
        )
        scores = jnp.dot(projected, right_half.T, preferred_element_type=jnp.float32)
        score_grad = ((jax.nn.sigmoid(scores) - targets[slot_index]) / block_len).astype(
            jnp.bfloat16
        )
        carried = jnp.dot(score_grad, right_half, preferred_element_type=jnp.float32).astype(
            jnp.bfloat16
        )
        grad_left = grad_left + jnp.dot(carried, matrix.T, preferred_element_type=jnp.float32)
        grad_right = grad_right + jnp.dot(
            score_grad.T, projected, preferred_element_type=jnp.float32
        )
        rel_grads.append(jnp.dot(left_half.T, carried, preferred_element_type=jnp.float32))
    left_new, left_st_new = adagrad(left_block, left_st, grad_left)
    right_new, right_st_new = adagrad(right_block, right_st, grad_right)
    return (left_new, left_st_new, right_new, right_st_new, rel_grads)


def partner_blocks(row_block, state_block, switch):
    count = lax.axis_size("bucket")

    def exchange(offset):
        pairs = [(b, b ^ offset) for b in range(count)]

        def run(rows, states):
            return (lax.ppermute(rows, "bucket", pairs), lax.ppermute(states, "bucket", pairs))

        return run

    branches = [exchange(offset) for offset in range(1, count)]
    return lax.switch(switch - 1, branches, row_block, state_block)


def axis_bits(axis):
    count = lax.axis_size(axis)
    return [1 << j for j in range(count.bit_length() - 1)]


def halving_sum(chunks, axis, order):
    count = lax.axis_size(axis)
    index = lax.axis_index(axis)
    current = chunks
    done = []
    for bit in order:
        lower = 1
        for other in axis_bits(axis):
            if other < bit and other not in done:
                lower *= 2
        upper = current.shape[0] // (2 * lower)
        split = current.reshape((upper, 2, lower) + current.shape[1:])
        mine = (index // bit) % 2
        keep = lax.dynamic_index_in_dim(split, mine, axis=1, keepdims=False)
        send = lax.dynamic_index_in_dim(split, 1 - mine, axis=1, keepdims=False)
        got = lax.ppermute(send, axis, [(k, k ^ bit) for k in range(count)])
        current = (keep + got).reshape((upper * lower,) + current.shape[1:])
        done.append(bit)
    return current[0]


def doubling_gather(piece, axis, order):
    count = lax.axis_size(axis)
    index = lax.axis_index(axis)
    current = piece[None]
    done = []
    for bit in order:
        lower = 1
        for other in done:
            if other < bit:
                lower *= 2
        upper = current.shape[0] // lower
        got = lax.ppermute(current, axis, [(k, k ^ bit) for k in range(count)])
        mine = (index // bit) % 2
        ours = current.reshape((upper, 1, lower) + piece.shape)
        theirs = got.reshape((upper, 1, lower) + piece.shape)
        joined = jnp.zeros((upper, 2, lower) + piece.shape, piece.dtype)
        joined = lax.dynamic_update_index_in_dim(joined, ours, mine, axis=1)
        joined = lax.dynamic_update_index_in_dim(joined, theirs, 1 - mine, axis=1)
        current = joined.reshape((upper * 2 * lower,) + piece.shape)
        done.append(bit)
    return current


def reduce_gradients(gradients, rel_ids, rel_total, width):
    stacked = jnp.stack(gradients)
    rel_list = jnp.arange(rel_total, dtype=jnp.int32)
    weights = (rel_ids[:, None] == rel_list[None, :]).astype(jnp.float32)
    term = jnp.einsum("sk,sde->kde", weights, stacked, precision=lax.Precision.HIGHEST)
    rel_count = lax.axis_size("rel")
    bucket_count = lax.axis_size("bucket")
    own = halving_sum(term.reshape(rel_count, -1, width), "rel", axis_bits("rel"))
    part = halving_sum(own.reshape(bucket_count, -1, width), "bucket", axis_bits("bucket"))
    return doubling_gather(part, "bucket", axis_bits("bucket")[::-1]).reshape(-1, width)


def on_device(
    left_rows,
    left_state,
    right_rows,
    right_state,
    relations,
    fetch_ids,
    edge_left,
    edge_right,
    edge_slot,
    edge_weight,
    matching,
):
    width = relations.shape[1]
    rel_table = doubling_gather(relations, "rel", axis_bits("rel")[::-1]).reshape(
        -1, width, width
    )
    rel_total = rel_table.shape[0]
    rel_ids = fetch_ids[0, 0]
    switch = matching[0]
    table_left, state_left = (left_rows, left_state)
    row_block, state_block = (right_rows, right_state)
    gradients = []
    for round_index in range(2):
        rel_pair = jnp.take(rel_table, rel_ids[2 * round_index : 2 * round_index + 2], axis=0)
        table_left, state_left, row_block, state_block, rel_grads = one_round(
            table_left,
            state_left,
            row_block,
            state_block,
            rel_pair,
            edge_left[0, 0, round_index],
            edge_right[0, 0, round_index],
            edge_slot[0, 0, round_index],
            edge_weight[0, 0, round_index],
        )
        gradients.extend(rel_grads)
        if round_index == 0:
            row_block, state_block = partner_blocks(row_block, state_block, switch)
    owned = reduce_gradients(gradients, rel_ids, rel_total, width)
    return (table_left, state_left, row_block, state_block, owned.reshape(-1, width, width))


def solution(mesh):
    in_specs = (
        P(("bucket", "rel"), None),
        P(("bucket", "rel")),
        P(("bucket", "rel"), None),
        P(("bucket", "rel")),
        P("rel", None, None),
        P("bucket", "rel", None),
        P("bucket", "rel", None, None),
        P("bucket", "rel", None, None),
        P("bucket", "rel", None, None),
        P("bucket", "rel", None, None),
        P(),
    )
    out_specs = (
        P(("bucket", "rel"), None),
        P(("bucket", "rel")),
        P(("bucket", "rel"), None),
        P(("bucket", "rel")),
        P("rel", None, None),
    )
    return jax.shard_map(
        on_device, mesh=mesh, in_specs=in_specs, out_specs=out_specs, check_vma=False
    )
```

```python
import jax
import jax.numpy as jnp
from jax import lax
from jax.sharding import PartitionSpec as P

learn_rate = 0.1


def edge_targets(edge_left, edge_right, edge_slot, edge_weight, block_len):
    rows = jnp.arange(block_len, dtype=jnp.int32)
    weight = edge_weight.astype(jnp.float32)
    right_hot = (edge_right[:, None] == rows[None, :]).astype(jnp.bfloat16)
    left_hot = edge_left[:, None] == rows[None, :]
    targets = []
    for slot_index in range(2):
        scale = jnp.where(edge_slot == slot_index, weight, jnp.float32(0.0))
        left_w = jnp.where(left_hot, scale[:, None], jnp.float32(0.0)).astype(jnp.bfloat16)
        targets.append(
            lax.dot_general(
                left_w, right_hot, (((0,), (0,)), ((), ())), preferred_element_type=jnp.float32
            )
        )
    return targets


def adagrad(table, state, gradient):
    state_new = state + jnp.mean(gradient * gradient, axis=1)
    return (table - learn_rate * gradient / jnp.sqrt(state_new)[:, None], state_new)


def one_round(
    left_block,
    left_st,
    right_block,
    right_st,
    rel_pair,
    edge_left,
    edge_right,
    edge_slot,
    edge_weight,
):
    block_len = left_block.shape[0]
    left_half = left_block.astype(jnp.bfloat16)
    right_half = right_block.astype(jnp.bfloat16)
    targets = edge_targets(edge_left, edge_right, edge_slot, edge_weight, block_len)
    grad_left = jnp.zeros(left_block.shape, jnp.float32)
    grad_right = jnp.zeros(right_block.shape, jnp.float32)
    rel_grads = []
    for slot_index in range(2):
        matrix = rel_pair[slot_index]
        projected = jnp.dot(left_half, matrix, preferred_element_type=jnp.float32).astype(
            jnp.bfloat16
        )
        scores = jnp.dot(projected, right_half.T, preferred_element_type=jnp.float32)
        score_grad = ((jax.nn.sigmoid(scores) - targets[slot_index]) / block_len).astype(
            jnp.bfloat16
        )
        carried = jnp.dot(score_grad, right_half, preferred_element_type=jnp.float32).astype(
            jnp.bfloat16
        )
        grad_left = grad_left + jnp.dot(carried, matrix.T, preferred_element_type=jnp.float32)
        grad_right = grad_right + jnp.dot(
            score_grad.T, projected, preferred_element_type=jnp.float32
        )
        rel_grads.append(jnp.dot(left_half.T, carried, preferred_element_type=jnp.float32))
    left_new, left_st_new = adagrad(left_block, left_st, grad_left)
    right_new, right_st_new = adagrad(right_block, right_st, grad_right)
    return (left_new, left_st_new, right_new, right_st_new, rel_grads)


def partner_blocks(row_block, state_block, switch):
    count = lax.axis_size("bucket")

    def exchange(offset):
        pairs = [(b, b ^ offset) for b in range(count)]

        def run(rows, states):
            return (lax.ppermute(rows, "bucket", pairs), lax.ppermute(states, "bucket", pairs))

        return run

    branches = [exchange(offset) for offset in range(1, count)]
    return lax.switch(switch - 1, branches, row_block, state_block)


def axis_bits(axis):
    count = lax.axis_size(axis)
    return [1 << j for j in range(count.bit_length() - 1)]


def halving_sum(chunks, axis, order, done=()):
    count = lax.axis_size(axis)
    index = lax.axis_index(axis)
    current = chunks
    done = list(done)
    for bit in order:
        lower = 1
        for other in axis_bits(axis):
            if other < bit and other not in done:
                lower *= 2
        upper = current.shape[0] // (2 * lower)
        split = current.reshape((upper, 2, lower) + current.shape[1:])
        mine = (index // bit) % 2
        keep = lax.dynamic_index_in_dim(split, mine, axis=1, keepdims=False)
        send = lax.dynamic_index_in_dim(split, 1 - mine, axis=1, keepdims=False)
        got = lax.ppermute(send, axis, [(k, k ^ bit) for k in range(count)])
        current = (keep + got).reshape((upper * lower,) + current.shape[1:])
        done.append(bit)
    return current[0]


def doubling_gather(piece, axis, order):
    count = lax.axis_size(axis)
    index = lax.axis_index(axis)
    current = piece[None]
    done = []
    for bit in order:
        lower = 1
        for other in done:
            if other < bit:
                lower *= 2
        upper = current.shape[0] // lower
        got = lax.ppermute(current, axis, [(k, k ^ bit) for k in range(count)])
        mine = (index // bit) % 2
        ours = current.reshape((upper, 1, lower) + piece.shape)
        theirs = got.reshape((upper, 1, lower) + piece.shape)
        joined = jnp.zeros((upper, 2, lower) + piece.shape, piece.dtype)
        joined = lax.dynamic_update_index_in_dim(joined, ours, mine, axis=1)
        joined = lax.dynamic_update_index_in_dim(joined, theirs, 1 - mine, axis=1)
        current = joined.reshape((upper * 2 * lower,) + piece.shape)
        done.append(bit)
    return current


def selected_term(gradients, rel_ids, devices, per_device, pieces):
    width = gradients[0].shape[0]
    wanted = devices[:, None] * per_device + jnp.arange(per_device, dtype=jnp.int32)[None, :]
    total = jnp.zeros((devices.shape[0], per_device, width, width), jnp.float32)
    for slot_index, gradient in enumerate(gradients):
        hit = (rel_ids[slot_index] == wanted)[:, :, None, None]
        total = total + jnp.where(hit, gradient[None, None], jnp.float32(0.0))
    rows = per_device * width
    total = total.reshape(devices.shape[0], pieces, rows // pieces, width)
    return jnp.transpose(total, (1, 0, 2, 3))


def reduce_gradients(gradients, rel_ids, rel_total, width):
    rel_count = lax.axis_size("rel")
    bucket_count = lax.axis_size("bucket")
    per_device = rel_total // rel_count
    rel_bits = axis_bits("rel")
    first = rel_bits[0]
    mine = (lax.axis_index("rel") // first) % 2
    owners = jnp.arange(rel_count, dtype=jnp.int32).reshape(-1, 2, first)
    kept = lax.dynamic_index_in_dim(owners, mine, axis=1, keepdims=False).reshape(-1)
    sent = lax.dynamic_index_in_dim(owners, 1 - mine, axis=1, keepdims=False).reshape(-1)
    keep = selected_term(gradients, rel_ids, kept, per_device, bucket_count)
    send = selected_term(gradients, rel_ids, sent, per_device, bucket_count)
    got = lax.ppermute(send, "rel", [(k, k ^ first) for k in range(rel_count)])
    current = keep + got
    current = halving_sum(current, "bucket", axis_bits("bucket"))
    current = halving_sum(current, "rel", rel_bits[1:], done=(first,))
    return doubling_gather(current, "bucket", axis_bits("bucket")[::-1]).reshape(-1, width)


def on_device(
    left_rows,
    left_state,
    right_rows,
    right_state,
    relations,
    fetch_ids,
    edge_left,
    edge_right,
    edge_slot,
    edge_weight,
    matching,
):
    width = relations.shape[1]
    rel_table = doubling_gather(relations, "rel", axis_bits("rel")[::-1]).reshape(
        -1, width, width
    )
    rel_total = rel_table.shape[0]
    rel_ids = fetch_ids[0, 0]
    switch = matching[0]
    table_left, state_left = (left_rows, left_state)
    row_block, state_block = (right_rows, right_state)
    gradients = []
    for round_index in range(2):
        rel_pair = jnp.take(rel_table, rel_ids[2 * round_index : 2 * round_index + 2], axis=0)
        table_left, state_left, row_block, state_block, rel_grads = one_round(
            table_left,
            state_left,
            row_block,
            state_block,
            rel_pair,
            edge_left[0, 0, round_index],
            edge_right[0, 0, round_index],
            edge_slot[0, 0, round_index],
            edge_weight[0, 0, round_index],
        )
        gradients.extend(rel_grads)
        if round_index == 0:
            row_block, state_block = partner_blocks(row_block, state_block, switch)
    owned = reduce_gradients(gradients, rel_ids, rel_total, width)
    return (table_left, state_left, row_block, state_block, owned.reshape(-1, width, width))


def solution(mesh):
    in_specs = (
        P(("bucket", "rel"), None),
        P(("bucket", "rel")),
        P(("bucket", "rel"), None),
        P(("bucket", "rel")),
        P("rel", None, None),
        P("bucket", "rel", None),
        P("bucket", "rel", None, None),
        P("bucket", "rel", None, None),
        P("bucket", "rel", None, None),
        P("bucket", "rel", None, None),
        P(),
    )
    out_specs = (
        P(("bucket", "rel"), None),
        P(("bucket", "rel")),
        P(("bucket", "rel"), None),
        P(("bucket", "rel")),
        P("rel", None, None),
    )
    return jax.shard_map(
        on_device, mesh=mesh, in_specs=in_specs, out_specs=out_specs, check_vma=False
    )
```

```python
import jax
import jax.numpy as jnp
from jax import lax
from jax.sharding import PartitionSpec as P

learn_rate = 0.1


def edge_targets(edge_left, edge_right, edge_slot, edge_weight, block_len):
    rows = jnp.arange(block_len, dtype=jnp.int32)
    weight = edge_weight.astype(jnp.float32)
    right_hot = (edge_right[:, None] == rows[None, :]).astype(jnp.bfloat16)
    left_hot = edge_left[:, None] == rows[None, :]
    targets = []
    for slot_index in range(2):
        scale = jnp.where(edge_slot == slot_index, weight, jnp.float32(0.0))
        left_w = jnp.where(left_hot, scale[:, None], jnp.float32(0.0)).astype(jnp.bfloat16)
        targets.append(
            lax.dot_general(
                left_w, right_hot, (((0,), (0,)), ((), ())), preferred_element_type=jnp.float32
            )
        )
    return targets


def adagrad(table, state, gradient):
    state_new = state + jnp.mean(gradient * gradient, axis=1)
    return (table - learn_rate * gradient / jnp.sqrt(state_new)[:, None], state_new)


def one_round(
    left_block,
    left_st,
    right_block,
    right_st,
    rel_pair,
    edge_left,
    edge_right,
    edge_slot,
    edge_weight,
):
    block_len = left_block.shape[0]
    left_half = left_block.astype(jnp.bfloat16)
    right_half = right_block.astype(jnp.bfloat16)
    targets = edge_targets(edge_left, edge_right, edge_slot, edge_weight, block_len)
    grad_left = jnp.zeros(left_block.shape, jnp.float32)
    grad_right = jnp.zeros(right_block.shape, jnp.float32)
    rel_grads = []
    for slot_index in range(2):
        matrix = rel_pair[slot_index]
        projected = jnp.dot(left_half, matrix, preferred_element_type=jnp.float32).astype(
            jnp.bfloat16
        )
        scores = jnp.dot(projected, right_half.T, preferred_element_type=jnp.float32)
        score_grad = ((jax.nn.sigmoid(scores) - targets[slot_index]) / block_len).astype(
            jnp.bfloat16
        )
        carried = jnp.dot(score_grad, right_half, preferred_element_type=jnp.float32).astype(
            jnp.bfloat16
        )
        grad_left = grad_left + jnp.dot(carried, matrix.T, preferred_element_type=jnp.float32)
        grad_right = grad_right + jnp.dot(
            score_grad.T, projected, preferred_element_type=jnp.float32
        )
        rel_grads.append(jnp.dot(left_half.T, carried, preferred_element_type=jnp.float32))
    left_new, left_st_new = adagrad(left_block, left_st, grad_left)
    right_new, right_st_new = adagrad(right_block, right_st, grad_right)
    return (left_new, left_st_new, right_new, right_st_new, rel_grads)


def partner_blocks(row_block, state_block, switch):
    count = lax.axis_size("bucket")

    def exchange(offset):
        pairs = [(b, b ^ offset) for b in range(count)]

        def run(rows, states):
            return (lax.ppermute(rows, "bucket", pairs), lax.ppermute(states, "bucket", pairs))

        return run

    branches = [exchange(offset) for offset in range(1, count)]
    return lax.switch(switch - 1, branches, row_block, state_block)


def axis_bits(axis):
    count = lax.axis_size(axis)
    return [1 << j for j in range(count.bit_length() - 1)]


def halving_sum(chunks, axis, order, done=()):
    count = lax.axis_size(axis)
    index = lax.axis_index(axis)
    current = chunks
    done = list(done)
    for bit in order:
        lower = 1
        for other in axis_bits(axis):
            if other < bit and other not in done:
                lower *= 2
        upper = current.shape[0] // (2 * lower)
        split = current.reshape((upper, 2, lower) + current.shape[1:])
        mine = (index // bit) % 2
        keep = lax.dynamic_index_in_dim(split, mine, axis=1, keepdims=False)
        send = lax.dynamic_index_in_dim(split, 1 - mine, axis=1, keepdims=False)
        got = lax.ppermute(send, axis, [(k, k ^ bit) for k in range(count)])
        current = (keep + got).reshape((upper * lower,) + current.shape[1:])
        done.append(bit)
    return current[0]


def doubling_gather(piece, axis, order):
    count = lax.axis_size(axis)
    index = lax.axis_index(axis)
    current = piece[None]
    done = []
    for bit in order:
        lower = 1
        for other in done:
            if other < bit:
                lower *= 2
        upper = current.shape[0] // lower
        got = lax.ppermute(current, axis, [(k, k ^ bit) for k in range(count)])
        mine = (index // bit) % 2
        ours = current.reshape((upper, 1, lower) + piece.shape)
        theirs = got.reshape((upper, 1, lower) + piece.shape)
        joined = jnp.zeros((upper, 2, lower) + piece.shape, piece.dtype)
        joined = lax.dynamic_update_index_in_dim(joined, ours, mine, axis=1)
        joined = lax.dynamic_update_index_in_dim(joined, theirs, 1 - mine, axis=1)
        current = joined.reshape((upper * 2 * lower,) + piece.shape)
        done.append(bit)
    return current


def selected_term(gradients, rel_ids, devices, per_device, pieces, columns):
    width = gradients[0].shape[0]
    wanted = devices[:, None] * per_device + jnp.arange(per_device, dtype=jnp.int32)[None, :]
    total = jnp.zeros((devices.shape[0], per_device, width, columns.stop - columns.start), jnp.float32)
    for slot_index, gradient in enumerate(gradients):
        hit = (rel_ids[slot_index] == wanted)[:, :, None, None]
        total = total + jnp.where(hit, gradient[None, None, :, columns], jnp.float32(0.0))
    rows = per_device * width
    return total.reshape(devices.shape[0], pieces, rows // pieces, columns.stop - columns.start)


def split_bits(array, axis_names, bits_by_axis, order):
    lead = []
    shape = []
    for name in axis_names:
        bits = bits_by_axis[name]
        for bit in bits[::-1]:
            lead.append((name, bit))
            shape.append(2)
    array = array.reshape(tuple(shape) + array.shape[len(axis_names) :])
    perm = [lead.index(step) for step in order] + list(range(len(lead), array.ndim))
    return jnp.transpose(array, perm)


def halving_steps(current, order):
    for step_index, (name, bit) in enumerate(order):
        count = lax.axis_size(name)
        mine = (lax.axis_index(name) // bit) % 2
        keep = lax.dynamic_index_in_dim(current, mine, axis=0, keepdims=False)
        send = lax.dynamic_index_in_dim(current, 1 - mine, axis=0, keepdims=False)
        got = lax.ppermute(send, name, [(k, k ^ bit) for k in range(count)])
        current = keep + got
    return current


def doubling_steps(piece, name, order):
    count = lax.axis_size(name)
    current = piece
    dims = []
    for bit in order:
        got = lax.ppermute(current, name, [(k, k ^ bit) for k in range(count)])
        mine = (lax.axis_index(name) // bit) % 2
        current = jnp.where(mine == 0, jnp.stack([current, got]), jnp.stack([got, current]))
        dims = [bit] + dims
    natural = sorted(dims, reverse=True)
    current = jnp.transpose(current, [dims.index(bit) for bit in natural] + list(range(len(dims), current.ndim)))
    return current.reshape((-1,) + piece.shape[1:])


def reduce_gradients(gradients, rel_ids, rel_total, width):
    rel_count = lax.axis_size("rel")
    bucket_count = lax.axis_size("bucket")
    per_device = rel_total // rel_count
    rel_bits = axis_bits("rel")
    bucket_bits = axis_bits("bucket")
    first = rel_bits[0]
    mine = (lax.axis_index("rel") // first) % 2
    owners = jnp.arange(rel_count, dtype=jnp.int32).reshape(-1, 2, first)
    kept = lax.dynamic_index_in_dim(owners, mine, axis=1, keepdims=False).reshape(-1)
    sent = lax.dynamic_index_in_dim(owners, 1 - mine, axis=1, keepdims=False).reshape(-1)
    rest = rel_bits[1:]
    bits_by_axis = {"rel": rest, "bucket": bucket_bits}
    rel_steps = [("rel", bit) for bit in rest]
    bucket_steps = [("bucket", bit) for bit in bucket_bits]
    streams = [
        (bucket_steps + rel_steps, bucket_bits[::-1]),
        (rel_steps + bucket_steps, bucket_bits[:1] + bucket_bits[1:][::-1]),
    ]
    band = width // len(streams)
    outputs = []
    for stream_index, (order, gather_order) in enumerate(streams):
        columns = slice(stream_index * band, (stream_index + 1) * band)
        keep = selected_term(gradients, rel_ids, kept, per_device, bucket_count, columns)
        send = selected_term(gradients, rel_ids, sent, per_device, bucket_count, columns)
        got = lax.ppermute(send, "rel", [(k, k ^ first) for k in range(rel_count)])
        current = split_bits(keep + got, ("rel", "bucket"), bits_by_axis, order)
        current = halving_steps(current, order)
        outputs.append(doubling_steps(current, "bucket", gather_order))
    return jnp.concatenate(outputs, axis=1)


def on_device(
    left_rows,
    left_state,
    right_rows,
    right_state,
    relations,
    fetch_ids,
    edge_left,
    edge_right,
    edge_slot,
    edge_weight,
    matching,
):
    width = relations.shape[1]
    rel_table = doubling_gather(relations, "rel", axis_bits("rel")[::-1]).reshape(
        -1, width, width
    )
    rel_total = rel_table.shape[0]
    rel_ids = fetch_ids[0, 0]
    switch = matching[0]
    table_left, state_left = (left_rows, left_state)
    row_block, state_block = (right_rows, right_state)
    gradients = []
    for round_index in range(2):
        rel_pair = jnp.take(rel_table, rel_ids[2 * round_index : 2 * round_index + 2], axis=0)
        table_left, state_left, row_block, state_block, rel_grads = one_round(
            table_left,
            state_left,
            row_block,
            state_block,
            rel_pair,
            edge_left[0, 0, round_index],
            edge_right[0, 0, round_index],
            edge_slot[0, 0, round_index],
            edge_weight[0, 0, round_index],
        )
        gradients.extend(rel_grads)
        if round_index == 0:
            row_block, state_block = partner_blocks(row_block, state_block, switch)
    owned = reduce_gradients(gradients, rel_ids, rel_total, width)
    return (table_left, state_left, row_block, state_block, owned.reshape(-1, width, width))


def solution(mesh):
    in_specs = (
        P(("bucket", "rel"), None),
        P(("bucket", "rel")),
        P(("bucket", "rel"), None),
        P(("bucket", "rel")),
        P("rel", None, None),
        P("bucket", "rel", None),
        P("bucket", "rel", None, None),
        P("bucket", "rel", None, None),
        P("bucket", "rel", None, None),
        P("bucket", "rel", None, None),
        P(),
    )
    out_specs = (
        P(("bucket", "rel"), None),
        P(("bucket", "rel")),
        P(("bucket", "rel"), None),
        P(("bucket", "rel")),
        P("rel", None, None),
    )
    return jax.shard_map(
        on_device, mesh=mesh, in_specs=in_specs, out_specs=out_specs, check_vma=False
    )
```

```python
import jax
import jax.numpy as jnp
from jax import lax
from jax.sharding import PartitionSpec as P

learn_rate = 0.1


def edge_targets(edge_left, edge_right, edge_slot, edge_weight, block_len):
    rows = jnp.arange(block_len, dtype=jnp.int32)
    weight = edge_weight.astype(jnp.float32)
    right_hot = (edge_right[:, None] == rows[None, :]).astype(jnp.bfloat16)
    left_hot = edge_left[:, None] == rows[None, :]
    targets = []
    for slot_index in range(2):
        scale = jnp.where(edge_slot == slot_index, weight, jnp.float32(0.0))
        left_w = jnp.where(left_hot, scale[:, None], jnp.float32(0.0)).astype(jnp.bfloat16)
        targets.append(
            lax.dot_general(
                left_w, right_hot, (((0,), (0,)), ((), ())), preferred_element_type=jnp.float32
            )
        )
    return targets


def adagrad(table, state, gradient):
    state_new = state + jnp.mean(gradient * gradient, axis=1)
    return (table - learn_rate * gradient / jnp.sqrt(state_new)[:, None], state_new)


def one_round(
    left_block,
    left_st,
    right_block,
    right_st,
    rel_pair,
    edge_left,
    edge_right,
    edge_slot,
    edge_weight,
):
    block_len = left_block.shape[0]
    left_half = left_block.astype(jnp.bfloat16)
    right_half = right_block.astype(jnp.bfloat16)
    targets = edge_targets(edge_left, edge_right, edge_slot, edge_weight, block_len)
    grad_left = jnp.zeros(left_block.shape, jnp.float32)
    grad_right = jnp.zeros(right_block.shape, jnp.float32)
    rel_grads = []
    for slot_index in range(2):
        matrix = rel_pair[slot_index]
        projected = jnp.dot(left_half, matrix, preferred_element_type=jnp.float32).astype(
            jnp.bfloat16
        )
        scores = jnp.dot(projected, right_half.T, preferred_element_type=jnp.float32)
        score_grad = ((jax.nn.sigmoid(scores) - targets[slot_index]) / block_len).astype(
            jnp.bfloat16
        )
        carried = jnp.dot(score_grad, right_half, preferred_element_type=jnp.float32).astype(
            jnp.bfloat16
        )
        grad_left = grad_left + jnp.dot(carried, matrix.T, preferred_element_type=jnp.float32)
        grad_right = grad_right + jnp.dot(
            score_grad.T, projected, preferred_element_type=jnp.float32
        )
        rel_grads.append(jnp.dot(left_half.T, carried, preferred_element_type=jnp.float32))
    left_new, left_st_new = adagrad(left_block, left_st, grad_left)
    right_new, right_st_new = adagrad(right_block, right_st, grad_right)
    return (left_new, left_st_new, right_new, right_st_new, rel_grads)


def partner_blocks(row_block, state_block, switch):
    count = lax.axis_size("bucket")

    def exchange(offset):
        pairs = [(b, b ^ offset) for b in range(count)]

        def run(rows, states):
            return (lax.ppermute(rows, "bucket", pairs), lax.ppermute(states, "bucket", pairs))

        return run

    branches = [exchange(offset) for offset in range(1, count)]
    return lax.switch(switch - 1, branches, row_block, state_block)


def axis_bits(axis):
    count = lax.axis_size(axis)
    return [1 << j for j in range(count.bit_length() - 1)]


def halving_sum(chunks, axis, order, done=()):
    count = lax.axis_size(axis)
    index = lax.axis_index(axis)
    current = chunks
    done = list(done)
    for bit in order:
        lower = 1
        for other in axis_bits(axis):
            if other < bit and other not in done:
                lower *= 2
        upper = current.shape[0] // (2 * lower)
        split = current.reshape((upper, 2, lower) + current.shape[1:])
        mine = (index // bit) % 2
        keep = lax.dynamic_index_in_dim(split, mine, axis=1, keepdims=False)
        send = lax.dynamic_index_in_dim(split, 1 - mine, axis=1, keepdims=False)
        got = lax.ppermute(send, axis, [(k, k ^ bit) for k in range(count)])
        current = (keep + got).reshape((upper * lower,) + current.shape[1:])
        done.append(bit)
    return current[0]


def doubling_gather(piece, axis, order):
    count = lax.axis_size(axis)
    index = lax.axis_index(axis)
    current = piece[None]
    done = []
    for bit in order:
        lower = 1
        for other in done:
            if other < bit:
                lower *= 2
        upper = current.shape[0] // lower
        got = lax.ppermute(current, axis, [(k, k ^ bit) for k in range(count)])
        mine = (index // bit) % 2
        ours = current.reshape((upper, 1, lower) + piece.shape)
        theirs = got.reshape((upper, 1, lower) + piece.shape)
        joined = jnp.zeros((upper, 2, lower) + piece.shape, piece.dtype)
        joined = lax.dynamic_update_index_in_dim(joined, ours, mine, axis=1)
        joined = lax.dynamic_update_index_in_dim(joined, theirs, 1 - mine, axis=1)
        current = joined.reshape((upper * 2 * lower,) + piece.shape)
        done.append(bit)
    return current


def selected_term(gradients, rel_ids, devices, per_device, pieces, columns):
    width = gradients[0].shape[0]
    wanted = devices[:, None] * per_device + jnp.arange(per_device, dtype=jnp.int32)[None, :]
    total = jnp.zeros((devices.shape[0], per_device, width, columns.stop - columns.start), jnp.float32)
    for slot_index, gradient in enumerate(gradients):
        hit = (rel_ids[slot_index] == wanted)[:, :, None, None]
        total = total + jnp.where(hit, gradient[None, None, :, columns], jnp.float32(0.0))
    rows = per_device * width
    return total.reshape(devices.shape[0], pieces, rows // pieces, columns.stop - columns.start)


def split_bits(array, axis_names, bits_by_axis, order):
    lead = []
    shape = []
    for name in axis_names:
        bits = bits_by_axis[name]
        for bit in bits[::-1]:
            lead.append((name, bit))
            shape.append(2)
    array = array.reshape(tuple(shape) + array.shape[len(axis_names) :])
    perm = [lead.index(step) for step in order] + list(range(len(lead), array.ndim))
    return jnp.transpose(array, perm)


def halving_steps(current, order):
    for step_index, (name, bit) in enumerate(order):
        count = lax.axis_size(name)
        mine = (lax.axis_index(name) // bit) % 2
        keep = lax.dynamic_index_in_dim(current, mine, axis=0, keepdims=False)
        send = lax.dynamic_index_in_dim(current, 1 - mine, axis=0, keepdims=False)
        got = lax.ppermute(send, name, [(k, k ^ bit) for k in range(count)])
        current = keep + got
    return current


def doubling_steps(piece, name, order):
    count = lax.axis_size(name)
    current = piece
    dims = []
    for bit in order:
        got = lax.ppermute(current, name, [(k, k ^ bit) for k in range(count)])
        mine = (lax.axis_index(name) // bit) % 2
        current = jnp.where(mine == 0, jnp.stack([current, got]), jnp.stack([got, current]))
        dims = [bit] + dims
    natural = sorted(dims, reverse=True)
    current = jnp.transpose(current, [dims.index(bit) for bit in natural] + list(range(len(dims), current.ndim)))
    return current.reshape((-1,) + piece.shape[1:])


def reduce_gradients(gradients, rel_ids, rel_total, width):
    rel_count = lax.axis_size("rel")
    bucket_count = lax.axis_size("bucket")
    per_device = rel_total // rel_count
    rel_bits = axis_bits("rel")
    bucket_bits = axis_bits("bucket")
    first = rel_bits[0]
    mine = (lax.axis_index("rel") // first) % 2
    owners = jnp.arange(rel_count, dtype=jnp.int32).reshape(-1, 2, first)
    kept = lax.dynamic_index_in_dim(owners, mine, axis=1, keepdims=False).reshape(-1)
    sent = lax.dynamic_index_in_dim(owners, 1 - mine, axis=1, keepdims=False).reshape(-1)
    rest = rel_bits[1:]
    bits_by_axis = {"rel": rest, "bucket": bucket_bits}
    rel_steps = [("rel", bit) for bit in rest]
    near = [("bucket", bucket_bits[0])]
    far = [("bucket", bit) for bit in bucket_bits[1:]]
    streams = [
        (1, near + far + rel_steps, bucket_bits[1:][::-1] + bucket_bits[:1]),
        (2, rel_steps + near + far, bucket_bits[:1] + bucket_bits[1:][::-1]),
        (1, far[:1] + rel_steps + near + far[1:], bucket_bits[1:] + bucket_bits[:1]),
    ]
    band = width // sum(share for share, _, _ in streams)
    outputs = []
    start = 0
    for share, order, gather_order in streams:
        columns = slice(start, start + share * band)
        start += share * band
        keep = selected_term(gradients, rel_ids, kept, per_device, bucket_count, columns)
        send = selected_term(gradients, rel_ids, sent, per_device, bucket_count, columns)
        got = lax.ppermute(send, "rel", [(k, k ^ first) for k in range(rel_count)])
        current = split_bits(keep + got, ("rel", "bucket"), bits_by_axis, order)
        current = halving_steps(current, order)
        outputs.append(doubling_steps(current, "bucket", gather_order))
    return jnp.concatenate(outputs, axis=1)


def on_device(
    left_rows,
    left_state,
    right_rows,
    right_state,
    relations,
    fetch_ids,
    edge_left,
    edge_right,
    edge_slot,
    edge_weight,
    matching,
):
    width = relations.shape[1]
    rel_table = doubling_gather(relations, "rel", axis_bits("rel")[::-1]).reshape(
        -1, width, width
    )
    rel_total = rel_table.shape[0]
    rel_ids = fetch_ids[0, 0]
    switch = matching[0]
    table_left, state_left = (left_rows, left_state)
    row_block, state_block = (right_rows, right_state)
    gradients = []
    for round_index in range(2):
        rel_pair = jnp.take(rel_table, rel_ids[2 * round_index : 2 * round_index + 2], axis=0)
        table_left, state_left, row_block, state_block, rel_grads = one_round(
            table_left,
            state_left,
            row_block,
            state_block,
            rel_pair,
            edge_left[0, 0, round_index],
            edge_right[0, 0, round_index],
            edge_slot[0, 0, round_index],
            edge_weight[0, 0, round_index],
        )
        gradients.extend(rel_grads)
        if round_index == 0:
            row_block, state_block = partner_blocks(row_block, state_block, switch)
    owned = reduce_gradients(gradients, rel_ids, rel_total, width)
    return (table_left, state_left, row_block, state_block, owned.reshape(-1, width, width))


def solution(mesh):
    in_specs = (
        P(("bucket", "rel"), None),
        P(("bucket", "rel")),
        P(("bucket", "rel"), None),
        P(("bucket", "rel")),
        P("rel", None, None),
        P("bucket", "rel", None),
        P("bucket", "rel", None, None),
        P("bucket", "rel", None, None),
        P("bucket", "rel", None, None),
        P("bucket", "rel", None, None),
        P(),
    )
    out_specs = (
        P(("bucket", "rel"), None),
        P(("bucket", "rel")),
        P(("bucket", "rel"), None),
        P(("bucket", "rel")),
        P("rel", None, None),
    )
    return jax.shard_map(
        on_device, mesh=mesh, in_specs=in_specs, out_specs=out_specs, check_vma=False
    )
```

```python
import jax
import jax.numpy as jnp
from jax import lax
from jax.sharding import PartitionSpec as P

learn_rate = 0.1


def edge_targets(edge_left, edge_right, edge_slot, edge_weight, block_len):
    rows = jnp.arange(block_len, dtype=jnp.int32)
    weight = edge_weight.astype(jnp.float32)
    right_hot = (edge_right[:, None] == rows[None, :]).astype(jnp.bfloat16)
    left_hot = edge_left[:, None] == rows[None, :]
    targets = []
    for slot_index in range(2):
        scale = jnp.where(edge_slot == slot_index, weight, jnp.float32(0.0))
        left_w = jnp.where(left_hot, scale[:, None], jnp.float32(0.0)).astype(jnp.bfloat16)
        targets.append(
            lax.dot_general(
                left_w, right_hot, (((0,), (0,)), ((), ())), preferred_element_type=jnp.float32
            )
        )
    return targets


def adagrad(table, state, gradient):
    state_new = state + jnp.mean(gradient * gradient, axis=1)
    return (table - learn_rate * gradient / jnp.sqrt(state_new)[:, None], state_new)


def one_round(
    left_block,
    left_st,
    right_block,
    right_st,
    rel_pair,
    edge_left,
    edge_right,
    edge_slot,
    edge_weight,
):
    block_len = left_block.shape[0]
    left_half = left_block.astype(jnp.bfloat16)
    right_half = right_block.astype(jnp.bfloat16)
    targets = edge_targets(edge_left, edge_right, edge_slot, edge_weight, block_len)
    grad_left = jnp.zeros(left_block.shape, jnp.float32)
    grad_right = jnp.zeros(right_block.shape, jnp.float32)
    rel_grads = []
    for slot_index in range(2):
        matrix = rel_pair[slot_index]
        projected = jnp.dot(left_half, matrix, preferred_element_type=jnp.float32).astype(
            jnp.bfloat16
        )
        scores = jnp.dot(projected, right_half.T, preferred_element_type=jnp.float32)
        score_grad = ((jax.nn.sigmoid(scores) - targets[slot_index]) / block_len).astype(
            jnp.bfloat16
        )
        carried = jnp.dot(score_grad, right_half, preferred_element_type=jnp.float32).astype(
            jnp.bfloat16
        )
        grad_left = grad_left + jnp.dot(carried, matrix.T, preferred_element_type=jnp.float32)
        grad_right = grad_right + jnp.dot(
            score_grad.T, projected, preferred_element_type=jnp.float32
        )
        rel_grads.append(jnp.dot(left_half.T, carried, preferred_element_type=jnp.float32))
    left_new, left_st_new = adagrad(left_block, left_st, grad_left)
    right_new, right_st_new = adagrad(right_block, right_st, grad_right)
    return (left_new, left_st_new, right_new, right_st_new, rel_grads)


def partner_blocks(row_block, state_block, switch):
    count = lax.axis_size("bucket")

    def exchange(offset):
        pairs = [(b, b ^ offset) for b in range(count)]

        def run(rows, states):
            return (lax.ppermute(rows, "bucket", pairs), lax.ppermute(states, "bucket", pairs))

        return run

    branches = [exchange(offset) for offset in range(1, count)]
    return lax.switch(switch - 1, branches, row_block, state_block)


def axis_bits(axis):
    count = lax.axis_size(axis)
    return [1 << j for j in range(count.bit_length() - 1)]


def halving_sum(chunks, axis, order, done=()):
    count = lax.axis_size(axis)
    index = lax.axis_index(axis)
    current = chunks
    done = list(done)
    for bit in order:
        lower = 1
        for other in axis_bits(axis):
            if other < bit and other not in done:
                lower *= 2
        upper = current.shape[0] // (2 * lower)
        split = current.reshape((upper, 2, lower) + current.shape[1:])
        mine = (index // bit) % 2
        keep = lax.dynamic_index_in_dim(split, mine, axis=1, keepdims=False)
        send = lax.dynamic_index_in_dim(split, 1 - mine, axis=1, keepdims=False)
        got = lax.ppermute(send, axis, [(k, k ^ bit) for k in range(count)])
        current = (keep + got).reshape((upper * lower,) + current.shape[1:])
        done.append(bit)
    return current[0]


def doubling_gather(piece, axis, order):
    count = lax.axis_size(axis)
    index = lax.axis_index(axis)
    current = piece[None]
    done = []
    for bit in order:
        lower = 1
        for other in done:
            if other < bit:
                lower *= 2
        upper = current.shape[0] // lower
        got = lax.ppermute(current, axis, [(k, k ^ bit) for k in range(count)])
        mine = (index // bit) % 2
        ours = current.reshape((upper, 1, lower) + piece.shape)
        theirs = got.reshape((upper, 1, lower) + piece.shape)
        joined = jnp.zeros((upper, 2, lower) + piece.shape, piece.dtype)
        joined = lax.dynamic_update_index_in_dim(joined, ours, mine, axis=1)
        joined = lax.dynamic_update_index_in_dim(joined, theirs, 1 - mine, axis=1)
        current = joined.reshape((upper * 2 * lower,) + piece.shape)
        done.append(bit)
    return current


def selected_term(gradients, rel_ids, devices, per_device, pieces, columns):
    width = gradients[0].shape[0]
    wanted = devices[:, None] * per_device + jnp.arange(per_device, dtype=jnp.int32)[None, :]
    total = jnp.zeros((devices.shape[0], per_device, width, columns.stop - columns.start), jnp.float32)
    for slot_index, gradient in enumerate(gradients):
        hit = (rel_ids[slot_index] == wanted)[:, :, None, None]
        total = total + jnp.where(hit, gradient[None, None, :, columns], jnp.float32(0.0))
    rows = per_device * width
    return total.reshape(devices.shape[0], pieces, rows // pieces, columns.stop - columns.start)


def split_bits(array, axis_names, bits_by_axis, order):
    lead = []
    shape = []
    for name in axis_names:
        for bit in bits_by_axis[name][::-1]:
            lead.append((name, bit))
            shape.append(2)
    array = array.reshape(tuple(shape) + array.shape[len(axis_names) :])
    perm = [lead.index(step) for step in order] + list(range(len(lead), array.ndim))
    return jnp.transpose(array, perm)


def exchange(arrays, steps, gathering):
    results = list(arrays)
    groups = {}
    for stream_index, step in enumerate(steps):
        groups.setdefault(step, []).append(stream_index)
    for (name, bit), members in groups.items():
        count = lax.axis_size(name)
        mine = (lax.axis_index(name) // bit) % 2
        pairs = [(k, k ^ bit) for k in range(count)]
        if gathering:
            sends = [arrays[i] for i in members]
        else:
            sends = [lax.dynamic_index_in_dim(arrays[i], 1 - mine, axis=0, keepdims=False) for i in members]
        got = lax.ppermute(jnp.stack(sends), name, pairs)
        for position, i in enumerate(members):
            if gathering:
                ours = arrays[i]
                results[i] = jnp.where(mine == 0, jnp.stack([ours, got[position]]), jnp.stack([got[position], ours]))
            else:
                keep = lax.dynamic_index_in_dim(arrays[i], mine, axis=0, keepdims=False)
                results[i] = keep + got[position]
    return results


def natural_rows(gathered, order):
    dims = order[::-1]
    natural = sorted(dims, reverse=True)
    perm = [dims.index(bit) for bit in natural] + list(range(len(dims), gathered.ndim))
    gathered = jnp.transpose(gathered, perm)
    return gathered.reshape((-1,) + gathered.shape[len(dims) + 1 :])


def reduce_gradients(gradients, rel_ids, rel_total, width):
    rel_count = lax.axis_size("rel")
    bucket_count = lax.axis_size("bucket")
    per_device = rel_total // rel_count
    rel_bits = axis_bits("rel")
    bucket_bits = axis_bits("bucket")
    first = rel_bits[0]
    mine = (lax.axis_index("rel") // first) % 2
    owners = jnp.arange(rel_count, dtype=jnp.int32).reshape(-1, 2, first)
    kept = lax.dynamic_index_in_dim(owners, mine, axis=1, keepdims=False).reshape(-1)
    sent = lax.dynamic_index_in_dim(owners, 1 - mine, axis=1, keepdims=False).reshape(-1)
    everything = slice(0, width)
    keep = selected_term(gradients, rel_ids, kept, per_device, bucket_count, everything)
    send = selected_term(gradients, rel_ids, sent, per_device, bucket_count, everything)
    got = lax.ppermute(send, "rel", [(k, k ^ first) for k in range(rel_count)])
    full = keep + got
    rest = rel_bits[1:]
    bits_by_axis = {"rel": rest, "bucket": bucket_bits}
    rel_steps = [("rel", bit) for bit in rest]
    near = [("bucket", bucket_bits[0])]
    far = [("bucket", bit) for bit in bucket_bits[1:]]
    orders = [rel_steps + near + far, rel_steps + far[:1] + near + far[1:]]
    gathers = [
        bucket_bits[1:][::-1] + bucket_bits[:1],
        bucket_bits[2:][::-1] + bucket_bits[:1] + bucket_bits[1:2],
    ]
    band = width // len(orders)
    currents = [
        split_bits(full[..., index * band : (index + 1) * band], ("rel", "bucket"), bits_by_axis, order)
        for index, order in enumerate(orders)
    ]
    for step_index in range(len(orders[0])):
        currents = exchange(currents, [order[step_index] for order in orders], False)
    for step_index in range(len(gathers[0])):
        steps = [("bucket", gather[step_index]) for gather in gathers]
        currents = exchange(currents, steps, True)
    outputs = [natural_rows(current, gather) for current, gather in zip(currents, gathers)]
    return jnp.concatenate(outputs, axis=1)


def on_device(
    left_rows,
    left_state,
    right_rows,
    right_state,
    relations,
    fetch_ids,
    edge_left,
    edge_right,
    edge_slot,
    edge_weight,
    matching,
):
    width = relations.shape[1]
    rel_table = doubling_gather(relations, "rel", axis_bits("rel")[::-1]).reshape(
        -1, width, width
    )
    rel_total = rel_table.shape[0]
    rel_ids = fetch_ids[0, 0]
    switch = matching[0]
    table_left, state_left = (left_rows, left_state)
    row_block, state_block = (right_rows, right_state)
    gradients = []
    for round_index in range(2):
        rel_pair = jnp.take(rel_table, rel_ids[2 * round_index : 2 * round_index + 2], axis=0)
        table_left, state_left, row_block, state_block, rel_grads = one_round(
            table_left,
            state_left,
            row_block,
            state_block,
            rel_pair,
            edge_left[0, 0, round_index],
            edge_right[0, 0, round_index],
            edge_slot[0, 0, round_index],
            edge_weight[0, 0, round_index],
        )
        gradients.extend(rel_grads)
        if round_index == 0:
            row_block, state_block = partner_blocks(row_block, state_block, switch)
    owned = reduce_gradients(gradients, rel_ids, rel_total, width)
    return (table_left, state_left, row_block, state_block, owned.reshape(-1, width, width))


def solution(mesh):
    in_specs = (
        P(("bucket", "rel"), None),
        P(("bucket", "rel")),
        P(("bucket", "rel"), None),
        P(("bucket", "rel")),
        P("rel", None, None),
        P("bucket", "rel", None),
        P("bucket", "rel", None, None),
        P("bucket", "rel", None, None),
        P("bucket", "rel", None, None),
        P("bucket", "rel", None, None),
        P(),
    )
    out_specs = (
        P(("bucket", "rel"), None),
        P(("bucket", "rel")),
        P(("bucket", "rel"), None),
        P(("bucket", "rel")),
        P("rel", None, None),
    )
    return jax.shard_map(
        on_device, mesh=mesh, in_specs=in_specs, out_specs=out_specs, check_vma=False
    )
```

```python
import jax
import jax.numpy as jnp
from jax import lax
from jax.sharding import PartitionSpec as P

learn_rate = 0.1


def edge_targets(edge_left, edge_right, edge_slot, edge_weight, block_len):
    rows = jnp.arange(block_len, dtype=jnp.int32)
    weight = edge_weight.astype(jnp.float32)
    right_hot = (edge_right[:, None] == rows[None, :]).astype(jnp.bfloat16)
    left_hot = edge_left[:, None] == rows[None, :]
    targets = []
    for slot_index in range(2):
        scale = jnp.where(edge_slot == slot_index, weight, jnp.float32(0.0))
        left_w = jnp.where(left_hot, scale[:, None], jnp.float32(0.0)).astype(jnp.bfloat16)
        targets.append(
            lax.dot_general(
                left_w, right_hot, (((0,), (0,)), ((), ())), preferred_element_type=jnp.float32
            )
        )
    return targets


def adagrad(table, state, gradient):
    state_new = state + jnp.mean(gradient * gradient, axis=1)
    return (table - learn_rate * gradient / jnp.sqrt(state_new)[:, None], state_new)


def one_round(
    left_block,
    left_st,
    right_block,
    right_st,
    rel_pair,
    edge_left,
    edge_right,
    edge_slot,
    edge_weight,
):
    block_len = left_block.shape[0]
    left_half = left_block.astype(jnp.bfloat16)
    right_half = right_block.astype(jnp.bfloat16)
    targets = edge_targets(edge_left, edge_right, edge_slot, edge_weight, block_len)
    grad_left = jnp.zeros(left_block.shape, jnp.float32)
    grad_right = jnp.zeros(right_block.shape, jnp.float32)
    rel_grads = []
    for slot_index in range(2):
        matrix = rel_pair[slot_index]
        projected = jnp.dot(left_half, matrix, preferred_element_type=jnp.float32).astype(
            jnp.bfloat16
        )
        scores = jnp.dot(projected, right_half.T, preferred_element_type=jnp.float32)
        score_grad = ((jax.nn.sigmoid(scores) - targets[slot_index]) / block_len).astype(
            jnp.bfloat16
        )
        carried = jnp.dot(score_grad, right_half, preferred_element_type=jnp.float32).astype(
            jnp.bfloat16
        )
        grad_left = grad_left + jnp.dot(carried, matrix.T, preferred_element_type=jnp.float32)
        grad_right = grad_right + jnp.dot(
            score_grad.T, projected, preferred_element_type=jnp.float32
        )
        rel_grads.append(jnp.dot(left_half.T, carried, preferred_element_type=jnp.float32))
    left_new, left_st_new = adagrad(left_block, left_st, grad_left)
    right_new, right_st_new = adagrad(right_block, right_st, grad_right)
    return (left_new, left_st_new, right_new, right_st_new, rel_grads)


def scored(left_half, right_half, matrix, target, block_len):
    projected = jnp.dot(left_half, matrix, preferred_element_type=jnp.float32).astype(jnp.bfloat16)
    scores = jnp.dot(projected, right_half.T, preferred_element_type=jnp.float32)
    score_grad = ((jax.nn.sigmoid(scores) - target) / block_len).astype(jnp.bfloat16)
    return projected, score_grad


def left_round(left_block, left_st, right_half, rel_pair, targets):
    block_len = left_block.shape[0]
    left_half = left_block.astype(jnp.bfloat16)
    grad_left = jnp.zeros(left_block.shape, jnp.float32)
    rel_grads = []
    for slot_index in range(2):
        matrix = rel_pair[slot_index]
        _, score_grad = scored(left_half, right_half, matrix, targets[slot_index], block_len)
        carried = jnp.dot(score_grad, right_half, preferred_element_type=jnp.float32).astype(
            jnp.bfloat16
        )
        grad_left = grad_left + jnp.dot(carried, matrix.T, preferred_element_type=jnp.float32)
        rel_grads.append(jnp.dot(left_half.T, carried, preferred_element_type=jnp.float32))
    left_new, left_st_new = adagrad(left_block, left_st, grad_left)
    return left_new, left_st_new, rel_grads


def right_round(left_half, right_block, right_st, rel_pair, targets):
    block_len = right_block.shape[0]
    right_half = right_block.astype(jnp.bfloat16)
    grad_right = jnp.zeros(right_block.shape, jnp.float32)
    for slot_index in range(2):
        projected, score_grad = scored(
            left_half, right_half, rel_pair[slot_index], targets[slot_index], block_len
        )
        grad_right = grad_right + jnp.dot(
            score_grad.T, projected, preferred_element_type=jnp.float32
        )
    return adagrad(right_block, right_st, grad_right)


def partner_inputs(arrays, switch):
    count = lax.axis_size("bucket")

    def exchange(offset):
        pairs = [(b, b ^ offset) for b in range(count)]

        def run(*values):
            return tuple(lax.ppermute(value, "bucket", pairs) for value in values)

        return run

    branches = [exchange(offset) for offset in range(1, count)]
    return lax.switch(switch - 1, branches, *arrays)


def axis_bits(axis):
    count = lax.axis_size(axis)
    return [1 << j for j in range(count.bit_length() - 1)]


def halving_sum(chunks, axis, order, done=()):
    count = lax.axis_size(axis)
    index = lax.axis_index(axis)
    current = chunks
    done = list(done)
    for bit in order:
        lower = 1
        for other in axis_bits(axis):
            if other < bit and other not in done:
                lower *= 2
        upper = current.shape[0] // (2 * lower)
        split = current.reshape((upper, 2, lower) + current.shape[1:])
        mine = (index // bit) % 2
        keep = lax.dynamic_index_in_dim(split, mine, axis=1, keepdims=False)
        send = lax.dynamic_index_in_dim(split, 1 - mine, axis=1, keepdims=False)
        got = lax.ppermute(send, axis, [(k, k ^ bit) for k in range(count)])
        current = (keep + got).reshape((upper * lower,) + current.shape[1:])
        done.append(bit)
    return current[0]


def doubling_gather(piece, axis, order):
    count = lax.axis_size(axis)
    index = lax.axis_index(axis)
    current = piece[None]
    done = []
    for bit in order:
        lower = 1
        for other in done:
            if other < bit:
                lower *= 2
        upper = current.shape[0] // lower
        got = lax.ppermute(current, axis, [(k, k ^ bit) for k in range(count)])
        mine = (index // bit) % 2
        ours = current.reshape((upper, 1, lower) + piece.shape)
        theirs = got.reshape((upper, 1, lower) + piece.shape)
        joined = jnp.zeros((upper, 2, lower) + piece.shape, piece.dtype)
        joined = lax.dynamic_update_index_in_dim(joined, ours, mine, axis=1)
        joined = lax.dynamic_update_index_in_dim(joined, theirs, 1 - mine, axis=1)
        current = joined.reshape((upper * 2 * lower,) + piece.shape)
        done.append(bit)
    return current


def selected_term(gradients, rel_ids, devices, per_device, pieces, columns):
    width = gradients[0].shape[0]
    wanted = devices[:, None] * per_device + jnp.arange(per_device, dtype=jnp.int32)[None, :]
    total = jnp.zeros((devices.shape[0], per_device, width, columns.stop - columns.start), jnp.float32)
    for slot_index, gradient in enumerate(gradients):
        hit = (rel_ids[slot_index] == wanted)[:, :, None, None]
        total = total + jnp.where(hit, gradient[None, None, :, columns], jnp.float32(0.0))
    rows = per_device * width
    return total.reshape(devices.shape[0], pieces, rows // pieces, columns.stop - columns.start)


def split_bits(array, axis_names, bits_by_axis, order):
    lead = []
    shape = []
    for name in axis_names:
        bits = bits_by_axis[name]
        for bit in bits[::-1]:
            lead.append((name, bit))
            shape.append(2)
    array = array.reshape(tuple(shape) + array.shape[len(axis_names) :])
    perm = [lead.index(step) for step in order] + list(range(len(lead), array.ndim))
    return jnp.transpose(array, perm)


def halving_steps(current, order):
    for step_index, (name, bit) in enumerate(order):
        count = lax.axis_size(name)
        mine = (lax.axis_index(name) // bit) % 2
        keep = lax.dynamic_index_in_dim(current, mine, axis=0, keepdims=False)
        send = lax.dynamic_index_in_dim(current, 1 - mine, axis=0, keepdims=False)
        got = lax.ppermute(send, name, [(k, k ^ bit) for k in range(count)])
        current = keep + got
    return current


def doubling_steps(piece, name, order):
    count = lax.axis_size(name)
    current = piece
    dims = []
    for bit in order:
        got = lax.ppermute(current, name, [(k, k ^ bit) for k in range(count)])
        mine = (lax.axis_index(name) // bit) % 2
        current = jnp.where(mine == 0, jnp.stack([current, got]), jnp.stack([got, current]))
        dims = [bit] + dims
    natural = sorted(dims, reverse=True)
    current = jnp.transpose(current, [dims.index(bit) for bit in natural] + list(range(len(dims), current.ndim)))
    return current.reshape((-1,) + piece.shape[1:])


def reduce_gradients(gradients, rel_ids, rel_total, width):
    rel_count = lax.axis_size("rel")
    bucket_count = lax.axis_size("bucket")
    per_device = rel_total // rel_count
    rel_bits = axis_bits("rel")
    bucket_bits = axis_bits("bucket")
    first = rel_bits[0]
    mine = (lax.axis_index("rel") // first) % 2
    owners = jnp.arange(rel_count, dtype=jnp.int32).reshape(-1, 2, first)
    kept = lax.dynamic_index_in_dim(owners, mine, axis=1, keepdims=False).reshape(-1)
    sent = lax.dynamic_index_in_dim(owners, 1 - mine, axis=1, keepdims=False).reshape(-1)
    rest = rel_bits[1:]
    bits_by_axis = {"rel": rest, "bucket": bucket_bits}
    rel_steps = [("rel", bit) for bit in rest]
    bucket_steps = [("bucket", bit) for bit in bucket_bits]
    streams = [
        (bucket_steps + rel_steps, bucket_bits[::-1]),
        (rel_steps + bucket_steps, bucket_bits[:1] + bucket_bits[1:][::-1]),
    ]
    band = width // len(streams)
    outputs = []
    for stream_index, (order, gather_order) in enumerate(streams):
        columns = slice(stream_index * band, (stream_index + 1) * band)
        keep = selected_term(gradients, rel_ids, kept, per_device, bucket_count, columns)
        send = selected_term(gradients, rel_ids, sent, per_device, bucket_count, columns)
        got = lax.ppermute(send, "rel", [(k, k ^ first) for k in range(rel_count)])
        current = split_bits(keep + got, ("rel", "bucket"), bits_by_axis, order)
        current = halving_steps(current, order)
        outputs.append(doubling_steps(current, "bucket", gather_order))
    return jnp.concatenate(outputs, axis=1)


def on_device(
    left_rows,
    left_state,
    right_rows,
    right_state,
    relations,
    fetch_ids,
    edge_left,
    edge_right,
    edge_slot,
    edge_weight,
    matching,
):
    width = relations.shape[1]
    rel_table = doubling_gather(relations, "rel", axis_bits("rel")[::-1]).reshape(
        -1, width, width
    )
    rel_total = rel_table.shape[0]
    rel_ids = fetch_ids[0, 0]
    switch = matching[0]
    block_len = left_rows.shape[0]
    first_edges = jnp.stack(
        [edge_left[0, 0, 0], edge_right[0, 0, 0], edge_slot[0, 0, 0], edge_weight[0, 0, 0]]
    )
    ints = jnp.concatenate(
        [first_edges, jnp.zeros((1, first_edges.shape[1]), jnp.int32).at[0, : rel_ids.shape[0]].set(rel_ids)]
    )
    floats = jnp.concatenate(
        [right_rows, jnp.zeros((1, right_rows.shape[1]), jnp.float32).at[0, :block_len].set(right_state)]
    )
    left_half = left_rows.astype(jnp.bfloat16)
    their_floats, their_left, their_ints = partner_inputs((floats, left_half, ints), switch)
    their_ids = their_ints[4, : rel_ids.shape[0]]
    own_pair = jnp.take(rel_table, rel_ids[0:2], axis=0)
    own_targets = edge_targets(
        edge_left[0, 0, 0], edge_right[0, 0, 0], edge_slot[0, 0, 0], edge_weight[0, 0, 0], block_len
    )
    table_left, state_left, gradients = left_round(
        left_rows, left_state, right_rows.astype(jnp.bfloat16), own_pair, own_targets
    )
    their_pair = jnp.take(rel_table, their_ids[0:2], axis=0)
    their_targets = edge_targets(
        their_ints[0], their_ints[1], their_ints[2], their_ints[3], block_len
    )
    row_block, state_block = right_round(
        their_left, their_floats[:block_len], their_floats[block_len, :block_len], their_pair, their_targets
    )
    rel_pair = jnp.take(rel_table, rel_ids[2:4], axis=0)
    table_left, state_left, row_block, state_block, rel_grads = one_round(
        table_left,
        state_left,
        row_block,
        state_block,
        rel_pair,
        edge_left[0, 0, 1],
        edge_right[0, 0, 1],
        edge_slot[0, 0, 1],
        edge_weight[0, 0, 1],
    )
    gradients = gradients + rel_grads
    owned = reduce_gradients(gradients, rel_ids, rel_total, width)
    return (table_left, state_left, row_block, state_block, owned.reshape(-1, width, width))


def solution(mesh):
    in_specs = (
        P(("bucket", "rel"), None),
        P(("bucket", "rel")),
        P(("bucket", "rel"), None),
        P(("bucket", "rel")),
        P("rel", None, None),
        P("bucket", "rel", None),
        P("bucket", "rel", None, None),
        P("bucket", "rel", None, None),
        P("bucket", "rel", None, None),
        P("bucket", "rel", None, None),
        P(),
    )
    out_specs = (
        P(("bucket", "rel"), None),
        P(("bucket", "rel")),
        P(("bucket", "rel"), None),
        P(("bucket", "rel")),
        P("rel", None, None),
    )
    return jax.shard_map(
        on_device, mesh=mesh, in_specs=in_specs, out_specs=out_specs, check_vma=False
    )
```

```python
import jax
import jax.numpy as jnp
from jax import lax
from jax.sharding import PartitionSpec as P

learn_rate = 0.1


def edge_targets(edge_left, edge_right, edge_slot, edge_weight, block_len):
    rows = jnp.arange(block_len, dtype=jnp.int32)
    weight = edge_weight.astype(jnp.float32)
    right_hot = (edge_right[:, None] == rows[None, :]).astype(jnp.bfloat16)
    left_hot = edge_left[:, None] == rows[None, :]
    targets = []
    for slot_index in range(2):
        scale = jnp.where(edge_slot == slot_index, weight, jnp.float32(0.0))
        left_w = jnp.where(left_hot, scale[:, None], jnp.float32(0.0)).astype(jnp.bfloat16)
        targets.append(
            lax.dot_general(
                left_w, right_hot, (((0,), (0,)), ((), ())), preferred_element_type=jnp.float32
            )
        )
    return targets


def adagrad(table, state, gradient):
    state_new = state + jnp.mean(gradient * gradient, axis=1)
    return (table - learn_rate * gradient / jnp.sqrt(state_new)[:, None], state_new)


def one_round(
    left_block,
    left_st,
    right_block,
    right_st,
    right_half,
    rel_pair,
    edge_left,
    edge_right,
    edge_slot,
    edge_weight,
):
    block_len = left_block.shape[0]
    left_half = left_block.astype(jnp.bfloat16)
    targets = edge_targets(edge_left, edge_right, edge_slot, edge_weight, block_len)
    grad_left = jnp.zeros(left_block.shape, jnp.float32)
    grad_right = jnp.zeros(right_half.shape, jnp.float32)
    rel_grads = []
    for slot_index in range(2):
        matrix = rel_pair[slot_index]
        projected = jnp.dot(left_half, matrix, preferred_element_type=jnp.float32).astype(
            jnp.bfloat16
        )
        scores = jnp.dot(projected, right_half.T, preferred_element_type=jnp.float32)
        score_grad = ((jax.nn.sigmoid(scores) - targets[slot_index]) / block_len).astype(
            jnp.bfloat16
        )
        carried = jnp.dot(score_grad, right_half, preferred_element_type=jnp.float32).astype(
            jnp.bfloat16
        )
        grad_left = grad_left + jnp.dot(carried, matrix.T, preferred_element_type=jnp.float32)
        grad_right = grad_right + jnp.dot(
            score_grad.T, projected, preferred_element_type=jnp.float32
        )
        rel_grads.append(jnp.dot(left_half.T, carried, preferred_element_type=jnp.float32))
    left_new, left_st_new = adagrad(left_block, left_st, grad_left)
    if right_block is None:
        return (left_new, left_st_new, None, (right_st, grad_right), rel_grads)
    right_new, right_st_new = adagrad(right_block, right_st, grad_right)
    return (left_new, left_st_new, right_new, right_st_new, rel_grads)


def partner_values(values, switch):
    count = lax.axis_size("bucket")

    def exchange(offset):
        pairs = [(b, b ^ offset) for b in range(count)]

        def run(*arrays):
            return tuple(lax.ppermute(array, "bucket", pairs) for array in arrays)

        return run

    branches = [exchange(offset) for offset in range(1, count)]
    return lax.switch(switch - 1, branches, *values)


def axis_bits(axis):
    count = lax.axis_size(axis)
    return [1 << j for j in range(count.bit_length() - 1)]


def halving_sum(chunks, axis, order, done=()):
    count = lax.axis_size(axis)
    index = lax.axis_index(axis)
    current = chunks
    done = list(done)
    for bit in order:
        lower = 1
        for other in axis_bits(axis):
            if other < bit and other not in done:
                lower *= 2
        upper = current.shape[0] // (2 * lower)
        split = current.reshape((upper, 2, lower) + current.shape[1:])
        mine = (index // bit) % 2
        keep = lax.dynamic_index_in_dim(split, mine, axis=1, keepdims=False)
        send = lax.dynamic_index_in_dim(split, 1 - mine, axis=1, keepdims=False)
        got = lax.ppermute(send, axis, [(k, k ^ bit) for k in range(count)])
        current = (keep + got).reshape((upper * lower,) + current.shape[1:])
        done.append(bit)
    return current[0]


def doubling_gather(piece, axis, order):
    count = lax.axis_size(axis)
    index = lax.axis_index(axis)
    current = piece[None]
    done = []
    for bit in order:
        lower = 1
        for other in done:
            if other < bit:
                lower *= 2
        upper = current.shape[0] // lower
        got = lax.ppermute(current, axis, [(k, k ^ bit) for k in range(count)])
        mine = (index // bit) % 2
        ours = current.reshape((upper, 1, lower) + piece.shape)
        theirs = got.reshape((upper, 1, lower) + piece.shape)
        joined = jnp.zeros((upper, 2, lower) + piece.shape, piece.dtype)
        joined = lax.dynamic_update_index_in_dim(joined, ours, mine, axis=1)
        joined = lax.dynamic_update_index_in_dim(joined, theirs, 1 - mine, axis=1)
        current = joined.reshape((upper * 2 * lower,) + piece.shape)
        done.append(bit)
    return current


def selected_term(gradients, rel_ids, devices, per_device, pieces, columns):
    width = gradients[0].shape[0]
    wanted = devices[:, None] * per_device + jnp.arange(per_device, dtype=jnp.int32)[None, :]
    total = jnp.zeros((devices.shape[0], per_device, width, columns.stop - columns.start), jnp.float32)
    for slot_index, gradient in enumerate(gradients):
        hit = (rel_ids[slot_index] == wanted)[:, :, None, None]
        total = total + jnp.where(hit, gradient[None, None, :, columns], jnp.float32(0.0))
    rows = per_device * width
    return total.reshape(devices.shape[0], pieces, rows // pieces, columns.stop - columns.start)


def split_bits(array, axis_names, bits_by_axis, order):
    lead = []
    shape = []
    for name in axis_names:
        bits = bits_by_axis[name]
        for bit in bits[::-1]:
            lead.append((name, bit))
            shape.append(2)
    array = array.reshape(tuple(shape) + array.shape[len(axis_names) :])
    perm = [lead.index(step) for step in order] + list(range(len(lead), array.ndim))
    return jnp.transpose(array, perm)


def halving_steps(current, order):
    for step_index, (name, bit) in enumerate(order):
        count = lax.axis_size(name)
        mine = (lax.axis_index(name) // bit) % 2
        keep = lax.dynamic_index_in_dim(current, mine, axis=0, keepdims=False)
        send = lax.dynamic_index_in_dim(current, 1 - mine, axis=0, keepdims=False)
        got = lax.ppermute(send, name, [(k, k ^ bit) for k in range(count)])
        current = keep + got
    return current


def doubling_steps(piece, name, order):
    count = lax.axis_size(name)
    current = piece
    dims = []
    for bit in order:
        got = lax.ppermute(current, name, [(k, k ^ bit) for k in range(count)])
        mine = (lax.axis_index(name) // bit) % 2
        current = jnp.where(mine == 0, jnp.stack([current, got]), jnp.stack([got, current]))
        dims = [bit] + dims
    natural = sorted(dims, reverse=True)
    current = jnp.transpose(current, [dims.index(bit) for bit in natural] + list(range(len(dims), current.ndim)))
    return current.reshape((-1,) + piece.shape[1:])


def reduce_gradients(gradients, rel_ids, rel_total, width, low, switch):
    rel_count = lax.axis_size("rel")
    bucket_count = lax.axis_size("bucket")
    per_device = rel_total // rel_count
    rel_bits = axis_bits("rel")
    bucket_bits = axis_bits("bucket")
    first = rel_bits[0]
    mine = (lax.axis_index("rel") // first) % 2
    owners = jnp.arange(rel_count, dtype=jnp.int32).reshape(-1, 2, first)
    kept = lax.dynamic_index_in_dim(owners, mine, axis=1, keepdims=False).reshape(-1)
    sent = lax.dynamic_index_in_dim(owners, 1 - mine, axis=1, keepdims=False).reshape(-1)
    rest = rel_bits[1:]
    bits_by_axis = {"rel": rest, "bucket": bucket_bits}
    rel_steps = [("rel", bit) for bit in rest]
    bucket_steps = [("bucket", bit) for bit in bucket_bits]
    streams = [
        (bucket_steps + rel_steps, bucket_bits[::-1]),
        (rel_steps + bucket_steps, bucket_bits[:1] + bucket_bits[1:][::-1]),
    ]
    band = width // len(streams)
    keeps = []
    sends = []
    for stream_index, (order, _) in enumerate(streams):
        columns = slice(stream_index * band, (stream_index + 1) * band)
        keep = selected_term(gradients, rel_ids, kept, per_device, bucket_count, columns)
        send = selected_term(gradients, rel_ids, sent, per_device, bucket_count, columns)
        got = lax.ppermute(send, "rel", [(k, k ^ first) for k in range(rel_count)])
        current = split_bits(keep + got, ("rel", "bucket"), bits_by_axis, order)
        name, bit = order[0]
        side = (lax.axis_index(name) // bit) % 2
        keeps.append(lax.dynamic_index_in_dim(current, side, axis=0, keepdims=False))
        sends.append(lax.dynamic_index_in_dim(current, 1 - side, axis=0, keepdims=False))
    count = lax.axis_size("bucket")

    def first_step(offset):
        pairs = [(b, b ^ offset) for b in range(count)]

        def run(low_part, *parts):
            moved = []
            for (order, _), part in zip(streams, parts):
                name, bit = order[0]
                size = lax.axis_size(name)
                moved.append(lax.ppermute(part, name, [(k, k ^ bit) for k in range(size)]))
            return (lax.ppermute(low_part, "bucket", pairs),) + tuple(moved)

        return run

    results = lax.switch(
        switch - 1, [first_step(offset) for offset in range(1, count)], low, *sends
    )
    block_low = results[0]
    outputs = []
    for (order, gather_order), keep, got in zip(streams, keeps, results[1:]):
        current = halving_steps(keep + got, order[1:])
        outputs.append(doubling_steps(current, "bucket", gather_order))
    return jnp.concatenate(outputs, axis=1), block_low


def on_device(
    left_rows,
    left_state,
    right_rows,
    right_state,
    relations,
    fetch_ids,
    edge_left,
    edge_right,
    edge_slot,
    edge_weight,
    matching,
):
    width = relations.shape[1]
    rel_table = doubling_gather(relations, "rel", axis_bits("rel")[::-1]).reshape(
        -1, width, width
    )
    rel_total = rel_table.shape[0]
    rel_ids = fetch_ids[0, 0]
    switch = matching[0]
    table_left, state_left = (left_rows, left_state)
    row_block, state_block = (right_rows, right_state)
    gradients = []
    right_half = row_block.astype(jnp.bfloat16)
    for round_index in range(2):
        rel_pair = jnp.take(rel_table, rel_ids[2 * round_index : 2 * round_index + 2], axis=0)
        table_left, state_left, row_block, state_block, rel_grads = one_round(
            table_left,
            state_left,
            row_block,
            state_block,
            right_half,
            rel_pair,
            edge_left[0, 0, round_index],
            edge_right[0, 0, round_index],
            edge_slot[0, 0, round_index],
            edge_weight[0, 0, round_index],
        )
        gradients.extend(rel_grads)
        if round_index == 0:
            rounded = lax.reduce_precision(row_block, exponent_bits=8, mantissa_bits=7)
            high = rounded.astype(jnp.bfloat16)
            low = (row_block - rounded).astype(jnp.bfloat16)
            right_half, state_block = partner_values((high, state_block), switch)
            block_high = right_half
            row_block = None

    right_st, grad_right = state_block
    owned, their_low = reduce_gradients(gradients, rel_ids, rel_total, width, low, switch)
    row_block, state_block = adagrad(
        block_high.astype(jnp.float32) + their_low.astype(jnp.float32), right_st, grad_right
    )
    return (table_left, state_left, row_block, state_block, owned.reshape(-1, width, width))


def solution(mesh):
    in_specs = (
        P(("bucket", "rel"), None),
        P(("bucket", "rel")),
        P(("bucket", "rel"), None),
        P(("bucket", "rel")),
        P("rel", None, None),
        P("bucket", "rel", None),
        P("bucket", "rel", None, None),
        P("bucket", "rel", None, None),
        P("bucket", "rel", None, None),
        P("bucket", "rel", None, None),
        P(),
    )
    out_specs = (
        P(("bucket", "rel"), None),
        P(("bucket", "rel")),
        P(("bucket", "rel"), None),
        P(("bucket", "rel")),
        P("rel", None, None),
    )
    return jax.shard_map(
        on_device, mesh=mesh, in_specs=in_specs, out_specs=out_specs, check_vma=False
    )
```

```python
import jax
import jax.numpy as jnp
from jax import lax
from jax.sharding import PartitionSpec as P

learn_rate = 0.1


def edge_targets(edge_left, edge_right, edge_slot, edge_weight, block_len):
    rows = jnp.arange(block_len, dtype=jnp.int32)
    weight = edge_weight.astype(jnp.float32)
    right_hot = (edge_right[:, None] == rows[None, :]).astype(jnp.bfloat16)
    left_hot = edge_left[:, None] == rows[None, :]
    targets = []
    for slot_index in range(2):
        scale = jnp.where(edge_slot == slot_index, weight, jnp.float32(0.0))
        left_w = jnp.where(left_hot, scale[:, None], jnp.float32(0.0)).astype(jnp.bfloat16)
        targets.append(
            lax.dot_general(
                left_w, right_hot, (((0,), (0,)), ((), ())), preferred_element_type=jnp.float32
            )
        )
    return targets


def adagrad(table, state, gradient):
    state_new = state + jnp.mean(gradient * gradient, axis=1)
    return (table - learn_rate * gradient / jnp.sqrt(state_new)[:, None], state_new)


def one_round(
    left_block,
    left_st,
    right_block,
    right_st,
    right_half,
    rel_pair,
    edge_left,
    edge_right,
    edge_slot,
    edge_weight,
):
    block_len = left_block.shape[0]
    left_half = left_block.astype(jnp.bfloat16)
    targets = edge_targets(edge_left, edge_right, edge_slot, edge_weight, block_len)
    grad_left = jnp.zeros(left_block.shape, jnp.float32)
    grad_right = jnp.zeros(right_half.shape, jnp.float32)
    rel_grads = []
    for slot_index in range(2):
        matrix = rel_pair[slot_index]
        projected = jnp.dot(left_half, matrix, preferred_element_type=jnp.float32).astype(
            jnp.bfloat16
        )
        scores = jnp.dot(projected, right_half.T, preferred_element_type=jnp.float32)
        score_grad = ((jax.nn.sigmoid(scores) - targets[slot_index]) / block_len).astype(
            jnp.bfloat16
        )
        carried = jnp.dot(score_grad, right_half, preferred_element_type=jnp.float32).astype(
            jnp.bfloat16
        )
        grad_left = grad_left + jnp.dot(carried, matrix.T, preferred_element_type=jnp.float32)
        grad_right = grad_right + jnp.dot(
            score_grad.T, projected, preferred_element_type=jnp.float32
        )
        rel_grads.append(jnp.dot(left_half.T, carried, preferred_element_type=jnp.float32))
    left_new, left_st_new = adagrad(left_block, left_st, grad_left)
    if right_block is None:
        return (left_new, left_st_new, None, (right_st, grad_right), rel_grads)
    right_new, right_st_new = adagrad(right_block, right_st, grad_right)
    return (left_new, left_st_new, right_new, right_st_new, rel_grads)


def partner_values(values, switch):
    count = lax.axis_size("bucket")

    def exchange(offset):
        pairs = [(b, b ^ offset) for b in range(count)]

        def run(*arrays):
            return tuple(lax.ppermute(array, "bucket", pairs) for array in arrays)

        return run

    branches = [exchange(offset) for offset in range(1, count)]
    return lax.switch(switch - 1, branches, *values)


def axis_bits(axis):
    count = lax.axis_size(axis)
    return [1 << j for j in range(count.bit_length() - 1)]


def halving_sum(chunks, axis, order, done=()):
    count = lax.axis_size(axis)
    index = lax.axis_index(axis)
    current = chunks
    done = list(done)
    for bit in order:
        lower = 1
        for other in axis_bits(axis):
            if other < bit and other not in done:
                lower *= 2
        upper = current.shape[0] // (2 * lower)
        split = current.reshape((upper, 2, lower) + current.shape[1:])
        mine = (index // bit) % 2
        keep = lax.dynamic_index_in_dim(split, mine, axis=1, keepdims=False)
        send = lax.dynamic_index_in_dim(split, 1 - mine, axis=1, keepdims=False)
        got = lax.ppermute(send, axis, [(k, k ^ bit) for k in range(count)])
        current = (keep + got).reshape((upper * lower,) + current.shape[1:])
        done.append(bit)
    return current[0]


def doubling_gather(piece, axis, order):
    count = lax.axis_size(axis)
    index = lax.axis_index(axis)
    current = piece[None]
    done = []
    for bit in order:
        lower = 1
        for other in done:
            if other < bit:
                lower *= 2
        upper = current.shape[0] // lower
        got = lax.ppermute(current, axis, [(k, k ^ bit) for k in range(count)])
        mine = (index // bit) % 2
        ours = current.reshape((upper, 1, lower) + piece.shape)
        theirs = got.reshape((upper, 1, lower) + piece.shape)
        joined = jnp.zeros((upper, 2, lower) + piece.shape, piece.dtype)
        joined = lax.dynamic_update_index_in_dim(joined, ours, mine, axis=1)
        joined = lax.dynamic_update_index_in_dim(joined, theirs, 1 - mine, axis=1)
        current = joined.reshape((upper * 2 * lower,) + piece.shape)
        done.append(bit)
    return current


def selected_term(gradients, rel_ids, devices, per_device, pieces, columns):
    width = gradients[0].shape[0]
    wanted = devices[:, None] * per_device + jnp.arange(per_device, dtype=jnp.int32)[None, :]
    total = jnp.zeros((devices.shape[0], per_device, width, columns.stop - columns.start), jnp.float32)
    for slot_index, gradient in enumerate(gradients):
        hit = (rel_ids[slot_index] == wanted)[:, :, None, None]
        total = total + jnp.where(hit, gradient[None, None, :, columns], jnp.float32(0.0))
    rows = per_device * width
    return total.reshape(devices.shape[0], pieces, rows // pieces, columns.stop - columns.start)


def split_bits(array, axis_names, bits_by_axis, order):
    lead = []
    shape = []
    for name in axis_names:
        bits = bits_by_axis[name]
        for bit in bits[::-1]:
            lead.append((name, bit))
            shape.append(2)
    array = array.reshape(tuple(shape) + array.shape[len(axis_names) :])
    perm = [lead.index(step) for step in order] + list(range(len(lead), array.ndim))
    return jnp.transpose(array, perm)


def halving_steps(current, order):
    for step_index, (name, bit) in enumerate(order):
        count = lax.axis_size(name)
        mine = (lax.axis_index(name) // bit) % 2
        keep = lax.dynamic_index_in_dim(current, mine, axis=0, keepdims=False)
        send = lax.dynamic_index_in_dim(current, 1 - mine, axis=0, keepdims=False)
        got = lax.ppermute(send, name, [(k, k ^ bit) for k in range(count)])
        current = keep + got
    return current


def doubling_steps(piece, name, order):
    count = lax.axis_size(name)
    current = piece
    dims = []
    for bit in order:
        got = lax.ppermute(current, name, [(k, k ^ bit) for k in range(count)])
        mine = (lax.axis_index(name) // bit) % 2
        current = jnp.where(mine == 0, jnp.stack([current, got]), jnp.stack([got, current]))
        dims = [bit] + dims
    natural = sorted(dims, reverse=True)
    current = jnp.transpose(current, [dims.index(bit) for bit in natural] + list(range(len(dims), current.ndim)))
    return current.reshape((-1,) + piece.shape[1:])


def reduce_gradients(gradients, rel_ids, rel_total, width, low, switch):
    rel_count = lax.axis_size("rel")
    bucket_count = lax.axis_size("bucket")
    per_device = rel_total // rel_count
    rel_bits = axis_bits("rel")
    bucket_bits = axis_bits("bucket")
    first = rel_bits[0]
    mine = (lax.axis_index("rel") // first) % 2
    owners = jnp.arange(rel_count, dtype=jnp.int32).reshape(-1, 2, first)
    kept = lax.dynamic_index_in_dim(owners, mine, axis=1, keepdims=False).reshape(-1)
    sent = lax.dynamic_index_in_dim(owners, 1 - mine, axis=1, keepdims=False).reshape(-1)
    rest = rel_bits[1:]
    bits_by_axis = {"rel": rest, "bucket": bucket_bits}
    rel_steps = [("rel", bit) for bit in rest]
    bucket_steps = [("bucket", bit) for bit in bucket_bits]
    streams = [
        (bucket_steps + rel_steps, bucket_bits[::-1]),
        (rel_steps + bucket_steps, bucket_bits[:1] + bucket_bits[1:][::-1]),
    ]
    band = width // len(streams)
    everything = slice(0, width)
    keep = selected_term(gradients, rel_ids, kept, per_device, bucket_count, everything)
    send = selected_term(gradients, rel_ids, sent, per_device, bucket_count, everything)
    full = keep + lax.ppermute(send, "rel", [(k, k ^ first) for k in range(rel_count)])
    keeps = []
    sends = []
    for stream_index, (order, _) in enumerate(streams):
        part = full[..., stream_index * band : (stream_index + 1) * band]
        current = split_bits(part, ("rel", "bucket"), bits_by_axis, order)
        name, bit = order[0]
        side = (lax.axis_index(name) // bit) % 2
        keeps.append(lax.dynamic_index_in_dim(current, side, axis=0, keepdims=False))
        sends.append(lax.dynamic_index_in_dim(current, 1 - side, axis=0, keepdims=False))
    count = lax.axis_size("bucket")

    def first_step(offset):
        pairs = [(b, b ^ offset) for b in range(count)]

        def run(low_part, *parts):
            moved = []
            for (order, _), part in zip(streams, parts):
                name, bit = order[0]
                size = lax.axis_size(name)
                moved.append(lax.ppermute(part, name, [(k, k ^ bit) for k in range(size)]))
            return (lax.ppermute(low_part, "bucket", pairs),) + tuple(moved)

        return run

    results = lax.switch(
        switch - 1, [first_step(offset) for offset in range(1, count)], low, *sends
    )
    block_low = results[0]
    outputs = []
    for (order, gather_order), keep, got in zip(streams, keeps, results[1:]):
        current = halving_steps(keep + got, order[1:])
        outputs.append(doubling_steps(current, "bucket", gather_order))
    return jnp.concatenate(outputs, axis=1), block_low


def on_device(
    left_rows,
    left_state,
    right_rows,
    right_state,
    relations,
    fetch_ids,
    edge_left,
    edge_right,
    edge_slot,
    edge_weight,
    matching,
):
    width = relations.shape[1]
    rel_table = doubling_gather(relations, "rel", axis_bits("rel")[::-1]).reshape(
        -1, width, width
    )
    rel_total = rel_table.shape[0]
    rel_ids = fetch_ids[0, 0]
    switch = matching[0]
    table_left, state_left = (left_rows, left_state)
    row_block, state_block = (right_rows, right_state)
    gradients = []
    right_half = row_block.astype(jnp.bfloat16)
    for round_index in range(2):
        rel_pair = jnp.take(rel_table, rel_ids[2 * round_index : 2 * round_index + 2], axis=0)
        table_left, state_left, row_block, state_block, rel_grads = one_round(
            table_left,
            state_left,
            row_block,
            state_block,
            right_half,
            rel_pair,
            edge_left[0, 0, round_index],
            edge_right[0, 0, round_index],
            edge_slot[0, 0, round_index],
            edge_weight[0, 0, round_index],
        )
        gradients.extend(rel_grads)
        if round_index == 0:
            rounded = lax.reduce_precision(row_block, exponent_bits=8, mantissa_bits=7)
            high = rounded.astype(jnp.bfloat16)
            low = (row_block - rounded).astype(jnp.bfloat16)
            state_rounded = lax.reduce_precision(state_block, exponent_bits=8, mantissa_bits=7)
            state_pair = jnp.concatenate([state_rounded, state_block - state_rounded])
            block_len, row_width = high.shape
            state_rows = -(-state_pair.shape[0] // row_width)
            state_pair = jnp.pad(state_pair, (0, state_rows * row_width - state_pair.shape[0]))
            packed = jnp.concatenate(
                [high, state_pair.astype(jnp.bfloat16).reshape(state_rows, row_width)]
            )
            (their_packed,) = partner_values((packed,), switch)
            right_half = their_packed[:block_len]
            their_state = their_packed[block_len:].reshape(-1).astype(jnp.float32)
            state_block = their_state[:block_len] + their_state[block_len : 2 * block_len]
            block_high = right_half
            row_block = None

    right_st, grad_right = state_block
    owned, their_low = reduce_gradients(gradients, rel_ids, rel_total, width, low, switch)
    row_block, state_block = adagrad(
        block_high.astype(jnp.float32) + their_low.astype(jnp.float32), right_st, grad_right
    )
    return (table_left, state_left, row_block, state_block, owned.reshape(-1, width, width))


def solution(mesh):
    in_specs = (
        P(("bucket", "rel"), None),
        P(("bucket", "rel")),
        P(("bucket", "rel"), None),
        P(("bucket", "rel")),
        P("rel", None, None),
        P("bucket", "rel", None),
        P("bucket", "rel", None, None),
        P("bucket", "rel", None, None),
        P("bucket", "rel", None, None),
        P("bucket", "rel", None, None),
        P(),
    )
    out_specs = (
        P(("bucket", "rel"), None),
        P(("bucket", "rel")),
        P(("bucket", "rel"), None),
        P(("bucket", "rel")),
        P("rel", None, None),
    )
    return jax.shard_map(
        on_device, mesh=mesh, in_specs=in_specs, out_specs=out_specs, check_vma=False
    )
```

```python
import jax
import jax.numpy as jnp
from jax import lax
from jax.sharding import PartitionSpec as P

learn_rate = 0.1


def edge_targets(edge_left, edge_right, edge_slot, edge_weight, block_len):
    rows = jnp.arange(block_len, dtype=jnp.int32)
    weight = edge_weight.astype(jnp.float32)
    right_hot = (edge_right[:, None] == rows[None, :]).astype(jnp.bfloat16)
    left_hot = edge_left[:, None] == rows[None, :]
    targets = []
    for slot_index in range(2):
        scale = jnp.where(edge_slot == slot_index, weight, jnp.float32(0.0))
        left_w = jnp.where(left_hot, scale[:, None], jnp.float32(0.0)).astype(jnp.bfloat16)
        targets.append(
            lax.dot_general(
                left_w, right_hot, (((0,), (0,)), ((), ())), preferred_element_type=jnp.float32
            )
        )
    return targets


def adagrad(table, state, gradient):
    state_new = state + jnp.mean(gradient * gradient, axis=1)
    return (table - learn_rate * gradient / jnp.sqrt(state_new)[:, None], state_new)


def one_round(
    left_block,
    left_st,
    right_block,
    right_st,
    right_half,
    rel_pair,
    edge_left,
    edge_right,
    edge_slot,
    edge_weight,
):
    block_len = left_block.shape[0]
    left_half = left_block.astype(jnp.bfloat16)
    targets = edge_targets(edge_left, edge_right, edge_slot, edge_weight, block_len)
    grad_left = jnp.zeros(left_block.shape, jnp.float32)
    grad_right = jnp.zeros(right_half.shape, jnp.float32)
    rel_grads = []
    for slot_index in range(2):
        matrix = rel_pair[slot_index]
        projected = jnp.dot(left_half, matrix, preferred_element_type=jnp.float32).astype(
            jnp.bfloat16
        )
        scores = jnp.dot(projected, right_half.T, preferred_element_type=jnp.float32)
        score_grad = ((jax.nn.sigmoid(scores) - targets[slot_index]) / block_len).astype(
            jnp.bfloat16
        )
        carried = jnp.dot(score_grad, right_half, preferred_element_type=jnp.float32).astype(
            jnp.bfloat16
        )
        grad_left = grad_left + jnp.dot(carried, matrix.T, preferred_element_type=jnp.float32)
        grad_right = grad_right + jnp.dot(
            score_grad.T, projected, preferred_element_type=jnp.float32
        )
        rel_grads.append(jnp.dot(left_half.T, carried, preferred_element_type=jnp.float32))
    left_new, left_st_new = adagrad(left_block, left_st, grad_left)
    if right_block is None:
        return (left_new, left_st_new, None, (right_st, grad_right), rel_grads)
    right_new, right_st_new = adagrad(right_block, right_st, grad_right)
    return (left_new, left_st_new, right_new, right_st_new, rel_grads)


def partner_values(values, switch):
    count = lax.axis_size("bucket")

    def exchange(offset):
        pairs = [(b, b ^ offset) for b in range(count)]

        def run(*arrays):
            return tuple(lax.ppermute(array, "bucket", pairs) for array in arrays)

        return run

    branches = [exchange(offset) for offset in range(1, count)]
    return lax.switch(switch - 1, branches, *values)


def axis_bits(axis):
    count = lax.axis_size(axis)
    return [1 << j for j in range(count.bit_length() - 1)]


def halving_sum(chunks, axis, order, done=()):
    count = lax.axis_size(axis)
    index = lax.axis_index(axis)
    current = chunks
    done = list(done)
    for bit in order:
        lower = 1
        for other in axis_bits(axis):
            if other < bit and other not in done:
                lower *= 2
        upper = current.shape[0] // (2 * lower)
        split = current.reshape((upper, 2, lower) + current.shape[1:])
        mine = (index // bit) % 2
        keep = lax.dynamic_index_in_dim(split, mine, axis=1, keepdims=False)
        send = lax.dynamic_index_in_dim(split, 1 - mine, axis=1, keepdims=False)
        got = lax.ppermute(send, axis, [(k, k ^ bit) for k in range(count)])
        current = (keep + got).reshape((upper * lower,) + current.shape[1:])
        done.append(bit)
    return current[0]


def doubling_gather(piece, axis, order):
    count = lax.axis_size(axis)
    index = lax.axis_index(axis)
    current = piece[None]
    done = []
    for bit in order:
        lower = 1
        for other in done:
            if other < bit:
                lower *= 2
        upper = current.shape[0] // lower
        got = lax.ppermute(current, axis, [(k, k ^ bit) for k in range(count)])
        mine = (index // bit) % 2
        ours = current.reshape((upper, 1, lower) + piece.shape)
        theirs = got.reshape((upper, 1, lower) + piece.shape)
        joined = jnp.zeros((upper, 2, lower) + piece.shape, piece.dtype)
        joined = lax.dynamic_update_index_in_dim(joined, ours, mine, axis=1)
        joined = lax.dynamic_update_index_in_dim(joined, theirs, 1 - mine, axis=1)
        current = joined.reshape((upper * 2 * lower,) + piece.shape)
        done.append(bit)
    return current


def selected_term(gradients, rel_ids, devices, per_device, pieces, columns):
    width = gradients[0].shape[0]
    wanted = devices[:, None] * per_device + jnp.arange(per_device, dtype=jnp.int32)[None, :]
    total = jnp.zeros((devices.shape[0], per_device, width, columns.stop - columns.start), jnp.float32)
    for slot_index, gradient in enumerate(gradients):
        hit = (rel_ids[slot_index] == wanted)[:, :, None, None]
        total = total + jnp.where(hit, gradient[None, None, :, columns], jnp.float32(0.0))
    rows = per_device * width
    return total.reshape(devices.shape[0], pieces, rows // pieces, columns.stop - columns.start)


def split_bits(array, axis_names, bits_by_axis, order):
    lead = []
    shape = []
    for name in axis_names:
        bits = bits_by_axis[name]
        for bit in bits[::-1]:
            lead.append((name, bit))
            shape.append(2)
    array = array.reshape(tuple(shape) + array.shape[len(axis_names) :])
    perm = [lead.index(step) for step in order] + list(range(len(lead), array.ndim))
    return jnp.transpose(array, perm)


def halving_steps(current, order):
    for step_index, (name, bit) in enumerate(order):
        count = lax.axis_size(name)
        mine = (lax.axis_index(name) // bit) % 2
        keep = lax.dynamic_index_in_dim(current, mine, axis=0, keepdims=False)
        send = lax.dynamic_index_in_dim(current, 1 - mine, axis=0, keepdims=False)
        got = lax.ppermute(send, name, [(k, k ^ bit) for k in range(count)])
        current = keep + got
    return current


def doubling_steps(piece, name, order):
    count = lax.axis_size(name)
    current = piece
    dims = []
    for bit in order:
        got = lax.ppermute(current, name, [(k, k ^ bit) for k in range(count)])
        mine = (lax.axis_index(name) // bit) % 2
        current = jnp.where(mine == 0, jnp.stack([current, got]), jnp.stack([got, current]))
        dims = [bit] + dims
    natural = sorted(dims, reverse=True)
    current = jnp.transpose(current, [dims.index(bit) for bit in natural] + list(range(len(dims), current.ndim)))
    return current.reshape((-1,) + piece.shape[1:])


def reduce_gradients(gradients, rel_ids, rel_total, width, low, switch):
    rel_count = lax.axis_size("rel")
    bucket_count = lax.axis_size("bucket")
    per_device = rel_total // rel_count
    rel_bits = axis_bits("rel")
    bucket_bits = axis_bits("bucket")
    first = rel_bits[0]
    mine = (lax.axis_index("rel") // first) % 2
    owners = jnp.arange(rel_count, dtype=jnp.int32).reshape(-1, 2, first)
    kept = lax.dynamic_index_in_dim(owners, mine, axis=1, keepdims=False).reshape(-1)
    sent = lax.dynamic_index_in_dim(owners, 1 - mine, axis=1, keepdims=False).reshape(-1)
    rest = rel_bits[1:]
    bits_by_axis = {"rel": rest, "bucket": bucket_bits}
    rel_steps = [("rel", bit) for bit in rest]
    bucket_steps = [("bucket", bit) for bit in bucket_bits]
    streams = [
        (bucket_steps + rel_steps, bucket_bits[::-1]),
        (rel_steps + bucket_steps, bucket_bits[:1] + bucket_bits[1:][::-1]),
    ]
    band = width // len(streams)
    everything = slice(0, width)
    keep = selected_term(gradients, rel_ids, kept, per_device, bucket_count, everything)
    send = selected_term(gradients, rel_ids, sent, per_device, bucket_count, everything)
    full = keep + lax.ppermute(send, "rel", [(k, k ^ first) for k in range(rel_count)])
    keeps = []
    sends = []
    for stream_index, (order, _) in enumerate(streams):
        part = full[..., stream_index * band : (stream_index + 1) * band]
        current = split_bits(part, ("rel", "bucket"), bits_by_axis, order)
        name, bit = order[0]
        side = (lax.axis_index(name) // bit) % 2
        keeps.append(lax.dynamic_index_in_dim(current, side, axis=0, keepdims=False))
        sends.append(lax.dynamic_index_in_dim(current, 1 - side, axis=0, keepdims=False))
    count = lax.axis_size("bucket")

    def first_step(offset):
        pairs = [(b, b ^ offset) for b in range(count)]

        def run(low_part, *parts):
            moved = []
            for (order, _), part in zip(streams, parts):
                name, bit = order[0]
                size = lax.axis_size(name)
                moved.append(lax.ppermute(part, name, [(k, k ^ bit) for k in range(size)]))
            return (lax.ppermute(low_part, "bucket", pairs),) + tuple(moved)

        return run

    results = lax.switch(
        switch - 1, [first_step(offset) for offset in range(1, count)], low, *sends
    )
    block_low = results[0]
    outputs = []
    for (order, gather_order), keep, got in zip(streams, keeps, results[1:]):
        current = halving_steps(keep + got, order[1:])
        outputs.append(doubling_steps(current, "bucket", gather_order))
    return jnp.concatenate(outputs, axis=1), block_low


def on_device(
    left_rows,
    left_state,
    right_rows,
    right_state,
    relations,
    fetch_ids,
    edge_left,
    edge_right,
    edge_slot,
    edge_weight,
    matching,
):
    width = relations.shape[1]
    rel_table = doubling_gather(relations, "rel", axis_bits("rel")[::-1]).reshape(
        -1, width, width
    )
    rel_total = rel_table.shape[0]
    rel_ids = fetch_ids[0, 0]
    switch = matching[0]
    table_left, state_left = (left_rows, left_state)
    row_block, state_block = (right_rows, right_state)
    gradients = []
    right_half = row_block.astype(jnp.bfloat16)
    for round_index in range(2):
        rel_pair = [
            lax.dynamic_index_in_dim(rel_table, rel_ids[2 * round_index + slot], 0, keepdims=False)
            for slot in range(2)
        ]
        table_left, state_left, row_block, state_block, rel_grads = one_round(
            table_left,
            state_left,
            row_block,
            state_block,
            right_half,
            rel_pair,
            edge_left[0, 0, round_index],
            edge_right[0, 0, round_index],
            edge_slot[0, 0, round_index],
            edge_weight[0, 0, round_index],
        )
        gradients.extend(rel_grads)
        if round_index == 0:
            rounded = lax.reduce_precision(row_block, exponent_bits=8, mantissa_bits=7)
            high = rounded.astype(jnp.bfloat16)
            low = (row_block - rounded).astype(jnp.bfloat16)
            state_rounded = lax.reduce_precision(state_block, exponent_bits=8, mantissa_bits=7)
            state_pair = jnp.concatenate([state_rounded, state_block - state_rounded])
            block_len, row_width = high.shape
            state_rows = -(-state_pair.shape[0] // row_width)
            state_pair = jnp.pad(state_pair, (0, state_rows * row_width - state_pair.shape[0]))
            packed = jnp.concatenate(
                [high, state_pair.astype(jnp.bfloat16).reshape(state_rows, row_width)]
            )
            (their_packed,) = partner_values((packed,), switch)
            right_half = their_packed[:block_len]
            their_state = their_packed[block_len:].reshape(-1).astype(jnp.float32)
            state_block = their_state[:block_len] + their_state[block_len : 2 * block_len]
            block_high = right_half
            row_block = None

    right_st, grad_right = state_block
    owned, their_low = reduce_gradients(gradients, rel_ids, rel_total, width, low, switch)
    row_block, state_block = adagrad(
        block_high.astype(jnp.float32) + their_low.astype(jnp.float32), right_st, grad_right
    )
    return (table_left, state_left, row_block, state_block, owned.reshape(-1, width, width))


def solution(mesh):
    in_specs = (
        P(("bucket", "rel"), None),
        P(("bucket", "rel")),
        P(("bucket", "rel"), None),
        P(("bucket", "rel")),
        P("rel", None, None),
        P("bucket", "rel", None),
        P("bucket", "rel", None, None),
        P("bucket", "rel", None, None),
        P("bucket", "rel", None, None),
        P("bucket", "rel", None, None),
        P(),
    )
    out_specs = (
        P(("bucket", "rel"), None),
        P(("bucket", "rel")),
        P(("bucket", "rel"), None),
        P(("bucket", "rel")),
        P("rel", None, None),
    )
    return jax.shard_map(
        on_device, mesh=mesh, in_specs=in_specs, out_specs=out_specs, check_vma=False
    )
```

```python
import jax
import jax.numpy as jnp
from jax import lax
from jax.sharding import PartitionSpec as P

learn_rate = 0.1


def edge_targets(edge_left, edge_right, edge_slot, edge_weight, block_len):
    rows = jnp.arange(block_len, dtype=jnp.int32)
    weight = edge_weight.astype(jnp.float32)
    right_hot = (edge_right[:, None] == rows[None, :]).astype(jnp.bfloat16)
    left_hot = edge_left[:, None] == rows[None, :]
    targets = []
    for slot_index in range(2):
        scale = jnp.where(edge_slot == slot_index, weight, jnp.float32(0.0))
        left_w = jnp.where(left_hot, scale[:, None], jnp.float32(0.0)).astype(jnp.bfloat16)
        targets.append(
            lax.dot_general(
                left_w, right_hot, (((0,), (0,)), ((), ())), preferred_element_type=jnp.float32
            )
        )
    return targets


def adagrad(table, state, gradient):
    state_new = state + jnp.mean(gradient * gradient, axis=1)
    return (table - learn_rate * gradient / jnp.sqrt(state_new)[:, None], state_new)


def one_round(
    left_block,
    left_st,
    right_block,
    right_st,
    right_half,
    rel_pair,
    edge_left,
    edge_right,
    edge_slot,
    edge_weight,
):
    block_len = left_block.shape[0]
    left_half = left_block.astype(jnp.bfloat16)
    targets = edge_targets(edge_left, edge_right, edge_slot, edge_weight, block_len)
    grad_left = jnp.zeros(left_block.shape, jnp.float32)
    grad_right = jnp.zeros(right_half.shape, jnp.float32)
    rel_grads = []
    for slot_index in range(2):
        matrix = rel_pair[slot_index]
        projected = jnp.dot(left_half, matrix, preferred_element_type=jnp.float32).astype(
            jnp.bfloat16
        )
        scores = jnp.dot(projected, right_half.T, preferred_element_type=jnp.float32)
        score_grad = ((jax.nn.sigmoid(scores) - targets[slot_index]) / block_len).astype(
            jnp.bfloat16
        )
        carried = jnp.dot(score_grad, right_half, preferred_element_type=jnp.float32).astype(
            jnp.bfloat16
        )
        grad_left = grad_left + jnp.dot(carried, matrix.T, preferred_element_type=jnp.float32)
        grad_right = grad_right + jnp.dot(
            score_grad.T, projected, preferred_element_type=jnp.float32
        )
        rel_grads.append(jnp.dot(left_half.T, carried, preferred_element_type=jnp.float32))
    left_new, left_st_new = adagrad(left_block, left_st, grad_left)
    if right_block is None:
        return (left_new, left_st_new, None, (right_st, grad_right), rel_grads)
    right_new, right_st_new = adagrad(right_block, right_st, grad_right)
    return (left_new, left_st_new, right_new, right_st_new, rel_grads)


def scored(left_half, right_half, matrix, target, block_len):
    projected = jnp.dot(left_half, matrix, preferred_element_type=jnp.float32).astype(jnp.bfloat16)
    scores = jnp.dot(projected, right_half.T, preferred_element_type=jnp.float32)
    score_grad = ((jax.nn.sigmoid(scores) - target) / block_len).astype(jnp.bfloat16)
    return projected, score_grad


def partner_values(values, switch):
    count = lax.axis_size("bucket")

    def exchange(offset):
        pairs = [(b, b ^ offset) for b in range(count)]

        def run(*arrays):
            return tuple(lax.ppermute(array, "bucket", pairs) for array in arrays)

        return run

    branches = [exchange(offset) for offset in range(1, count)]
    return lax.switch(switch - 1, branches, *values)


def axis_bits(axis):
    count = lax.axis_size(axis)
    return [1 << j for j in range(count.bit_length() - 1)]


def halving_sum(chunks, axis, order, done=()):
    count = lax.axis_size(axis)
    index = lax.axis_index(axis)
    current = chunks
    done = list(done)
    for bit in order:
        lower = 1
        for other in axis_bits(axis):
            if other < bit and other not in done:
                lower *= 2
        upper = current.shape[0] // (2 * lower)
        split = current.reshape((upper, 2, lower) + current.shape[1:])
        mine = (index // bit) % 2
        keep = lax.dynamic_index_in_dim(split, mine, axis=1, keepdims=False)
        send = lax.dynamic_index_in_dim(split, 1 - mine, axis=1, keepdims=False)
        got = lax.ppermute(send, axis, [(k, k ^ bit) for k in range(count)])
        current = (keep + got).reshape((upper * lower,) + current.shape[1:])
        done.append(bit)
    return current[0]


def doubling_gather(piece, axis, order):
    count = lax.axis_size(axis)
    index = lax.axis_index(axis)
    current = piece[None]
    done = []
    for bit in order:
        lower = 1
        for other in done:
            if other < bit:
                lower *= 2
        upper = current.shape[0] // lower
        got = lax.ppermute(current, axis, [(k, k ^ bit) for k in range(count)])
        mine = (index // bit) % 2
        ours = current.reshape((upper, 1, lower) + piece.shape)
        theirs = got.reshape((upper, 1, lower) + piece.shape)
        joined = jnp.zeros((upper, 2, lower) + piece.shape, piece.dtype)
        joined = lax.dynamic_update_index_in_dim(joined, ours, mine, axis=1)
        joined = lax.dynamic_update_index_in_dim(joined, theirs, 1 - mine, axis=1)
        current = joined.reshape((upper * 2 * lower,) + piece.shape)
        done.append(bit)
    return current


def selected_term(gradients, rel_ids, devices, per_device, pieces, columns):
    width = gradients[0].shape[0]
    wanted = devices[:, None] * per_device + jnp.arange(per_device, dtype=jnp.int32)[None, :]
    total = jnp.zeros((devices.shape[0], per_device, width, columns.stop - columns.start), jnp.float32)
    for slot_index, gradient in enumerate(gradients):
        hit = (rel_ids[slot_index] == wanted)[:, :, None, None]
        total = total + jnp.where(hit, gradient[None, None, :, columns], jnp.float32(0.0))
    rows = per_device * width
    return total.reshape(devices.shape[0], pieces, rows // pieces, columns.stop - columns.start)


def split_bits(array, axis_names, bits_by_axis, order):
    lead = []
    shape = []
    for name in axis_names:
        bits = bits_by_axis[name]
        for bit in bits[::-1]:
            lead.append((name, bit))
            shape.append(2)
    array = array.reshape(tuple(shape) + array.shape[len(axis_names) :])
    perm = [lead.index(step) for step in order] + list(range(len(lead), array.ndim))
    return jnp.transpose(array, perm)


def halving_steps(current, order):
    for step_index, (name, bit) in enumerate(order):
        count = lax.axis_size(name)
        mine = (lax.axis_index(name) // bit) % 2
        keep = lax.dynamic_index_in_dim(current, mine, axis=0, keepdims=False)
        send = lax.dynamic_index_in_dim(current, 1 - mine, axis=0, keepdims=False)
        got = lax.ppermute(send, name, [(k, k ^ bit) for k in range(count)])
        current = keep + got
    return current


def doubling_steps(piece, name, order):
    count = lax.axis_size(name)
    current = piece
    dims = []
    for bit in order:
        got = lax.ppermute(current, name, [(k, k ^ bit) for k in range(count)])
        mine = (lax.axis_index(name) // bit) % 2
        current = jnp.where(mine == 0, jnp.stack([current, got]), jnp.stack([got, current]))
        dims = [bit] + dims
    natural = sorted(dims, reverse=True)
    current = jnp.transpose(current, [dims.index(bit) for bit in natural] + list(range(len(dims), current.ndim)))
    return current.reshape((-1,) + piece.shape[1:])


def reduce_gradients(gradients, rel_ids, rel_total, width, low, switch):
    rel_count = lax.axis_size("rel")
    bucket_count = lax.axis_size("bucket")
    per_device = rel_total // rel_count
    rel_bits = axis_bits("rel")
    bucket_bits = axis_bits("bucket")
    first = rel_bits[0]
    mine = (lax.axis_index("rel") // first) % 2
    owners = jnp.arange(rel_count, dtype=jnp.int32).reshape(-1, 2, first)
    kept = lax.dynamic_index_in_dim(owners, mine, axis=1, keepdims=False).reshape(-1)
    sent = lax.dynamic_index_in_dim(owners, 1 - mine, axis=1, keepdims=False).reshape(-1)
    rest = rel_bits[1:]
    bits_by_axis = {"rel": rest, "bucket": bucket_bits}
    rel_steps = [("rel", bit) for bit in rest]
    bucket_steps = [("bucket", bit) for bit in bucket_bits]
    streams = [
        (bucket_steps + rel_steps, bucket_bits[::-1]),
        (rel_steps + bucket_steps, bucket_bits[:1] + bucket_bits[1:][::-1]),
    ]
    band = width // len(streams)
    everything = slice(0, width)
    keep = selected_term(gradients, rel_ids, kept, per_device, bucket_count, everything)
    send = selected_term(gradients, rel_ids, sent, per_device, bucket_count, everything)
    full = keep + lax.ppermute(send, "rel", [(k, k ^ first) for k in range(rel_count)])
    keeps = []
    sends = []
    for stream_index, (order, _) in enumerate(streams):
        part = full[..., stream_index * band : (stream_index + 1) * band]
        current = split_bits(part, ("rel", "bucket"), bits_by_axis, order)
        name, bit = order[0]
        side = (lax.axis_index(name) // bit) % 2
        keeps.append(lax.dynamic_index_in_dim(current, side, axis=0, keepdims=False))
        sends.append(lax.dynamic_index_in_dim(current, 1 - side, axis=0, keepdims=False))
    count = lax.axis_size("bucket")

    def first_step(offset):
        pairs = [(b, b ^ offset) for b in range(count)]

        def run(low_part, *parts):
            moved = []
            for (order, _), part in zip(streams, parts):
                name, bit = order[0]
                size = lax.axis_size(name)
                moved.append(lax.ppermute(part, name, [(k, k ^ bit) for k in range(size)]))
            return (lax.ppermute(low_part, "bucket", pairs),) + tuple(moved)

        return run

    results = lax.switch(
        switch - 1, [first_step(offset) for offset in range(1, count)], low, *sends
    )
    block_low = results[0]
    outputs = []
    for (order, gather_order), keep, got in zip(streams, keeps, results[1:]):
        current = halving_steps(keep + got, order[1:])
        outputs.append(doubling_steps(current, "bucket", gather_order))
    return jnp.concatenate(outputs, axis=1), block_low


def on_device(
    left_rows,
    left_state,
    right_rows,
    right_state,
    relations,
    fetch_ids,
    edge_left,
    edge_right,
    edge_slot,
    edge_weight,
    matching,
):
    width = relations.shape[1]
    rel_table = doubling_gather(relations, "rel", axis_bits("rel")[::-1]).reshape(
        -1, width, width
    )
    rel_total = rel_table.shape[0]
    rel_ids = fetch_ids[0, 0]
    switch = matching[0]
    table_left, state_left = (left_rows, left_state)
    row_block, state_block = (right_rows, right_state)
    block_len, row_width = right_rows.shape
    own_half = right_rows.astype(jnp.bfloat16)
    left_half = left_rows.astype(jnp.bfloat16)
    first_pair = jnp.take(rel_table, rel_ids[0:2], axis=0)
    targets = edge_targets(
        edge_left[0, 0, 0], edge_right[0, 0, 0], edge_slot[0, 0, 0], edge_weight[0, 0, 0], block_len
    )
    grad_right = jnp.zeros(right_rows.shape, jnp.float32)
    score_grads = []
    for slot_index in range(2):
        projected, score_grad = scored(
            left_half, own_half, first_pair[slot_index], targets[slot_index], block_len
        )
        score_grads.append(score_grad)
        grad_right = grad_right + jnp.dot(
            score_grad.T, projected, preferred_element_type=jnp.float32
        )
    right_new, right_st_new = adagrad(right_rows, right_state, grad_right)
    rounded = lax.reduce_precision(right_new, exponent_bits=8, mantissa_bits=7)
    high = rounded.astype(jnp.bfloat16)
    low = (right_new - rounded).astype(jnp.bfloat16)
    state_rounded = lax.reduce_precision(right_st_new, exponent_bits=8, mantissa_bits=7)
    state_pair = jnp.concatenate([state_rounded, right_st_new - state_rounded])
    state_rows = -(-state_pair.shape[0] // row_width)
    state_pair = jnp.pad(state_pair, (0, state_rows * row_width - state_pair.shape[0]))
    packed = jnp.concatenate([high, state_pair.astype(jnp.bfloat16).reshape(state_rows, row_width)])

    def left_side(left_block, left_st, matrices, grads_of_scores):
        grad_left = jnp.zeros(left_block.shape, jnp.float32)
        rel_grads = []
        for slot_index in range(2):
            carried = jnp.dot(
                grads_of_scores[slot_index], own_half, preferred_element_type=jnp.float32
            ).astype(jnp.bfloat16)
            grad_left = grad_left + jnp.dot(
                carried, matrices[slot_index].T, preferred_element_type=jnp.float32
            )
            rel_grads.append(jnp.dot(left_half.T, carried, preferred_element_type=jnp.float32))
        left_new, left_st_new = adagrad(left_block, left_st, grad_left)
        return (left_new, left_st_new) + tuple(rel_grads)

    count = lax.axis_size("bucket")

    def swap_and_update(offset):
        pairs = [(b, b ^ offset) for b in range(count)]

        def run(values, left_block, left_st, matrices, grads_of_scores):
            moved = lax.ppermute(values, "bucket", pairs)
            return (moved,) + left_side(left_block, left_st, matrices, grads_of_scores)

        return run

    outcome = lax.switch(
        switch - 1,
        [swap_and_update(offset) for offset in range(1, count)],
        packed,
        left_rows,
        left_state,
        first_pair,
        tuple(score_grads),
    )
    their_packed, table_left, state_left = outcome[:3]
    gradients = list(outcome[3:])
    right_half = their_packed[:block_len]
    their_state = their_packed[block_len:].reshape(-1).astype(jnp.float32)
    state_block = their_state[:block_len] + their_state[block_len : 2 * block_len]
    block_high = right_half
    rel_pair = jnp.take(rel_table, rel_ids[2:4], axis=0)
    table_left, state_left, _, state_block, rel_grads = one_round(
        table_left,
        state_left,
        None,
        state_block,
        right_half,
        rel_pair,
        edge_left[0, 0, 1],
        edge_right[0, 0, 1],
        edge_slot[0, 0, 1],
        edge_weight[0, 0, 1],
    )
    gradients.extend(rel_grads)
    right_st, grad_right = state_block
    owned, their_low = reduce_gradients(gradients, rel_ids, rel_total, width, low, switch)
    row_block, state_block = adagrad(
        block_high.astype(jnp.float32) + their_low.astype(jnp.float32), right_st, grad_right
    )
    return (table_left, state_left, row_block, state_block, owned.reshape(-1, width, width))


def solution(mesh):
    in_specs = (
        P(("bucket", "rel"), None),
        P(("bucket", "rel")),
        P(("bucket", "rel"), None),
        P(("bucket", "rel")),
        P("rel", None, None),
        P("bucket", "rel", None),
        P("bucket", "rel", None, None),
        P("bucket", "rel", None, None),
        P("bucket", "rel", None, None),
        P("bucket", "rel", None, None),
        P(),
    )
    out_specs = (
        P(("bucket", "rel"), None),
        P(("bucket", "rel")),
        P(("bucket", "rel"), None),
        P(("bucket", "rel")),
        P("rel", None, None),
    )
    return jax.shard_map(
        on_device, mesh=mesh, in_specs=in_specs, out_specs=out_specs, check_vma=False
    )
```

```python
import jax
import jax.numpy as jnp
from jax import lax
from jax.sharding import PartitionSpec as P

learn_rate = 0.1


def edge_targets(edge_left, edge_right, edge_slot, edge_weight, block_len):
    rows = jnp.arange(block_len, dtype=jnp.int32)
    weight = edge_weight.astype(jnp.float32)
    right_hot = (edge_right[:, None] == rows[None, :]).astype(jnp.bfloat16)
    left_hot = edge_left[:, None] == rows[None, :]
    targets = []
    for slot_index in range(2):
        scale = jnp.where(edge_slot == slot_index, weight, jnp.float32(0.0))
        left_w = jnp.where(left_hot, scale[:, None], jnp.float32(0.0)).astype(jnp.bfloat16)
        targets.append(
            lax.dot_general(
                left_w, right_hot, (((0,), (0,)), ((), ())), preferred_element_type=jnp.float32
            )
        )
    return targets


def adagrad(table, state, gradient):
    state_new = state + jnp.mean(gradient * gradient, axis=1)
    return (table - learn_rate * gradient / jnp.sqrt(state_new)[:, None], state_new)


def one_round(
    left_block,
    left_st,
    right_block,
    right_st,
    right_half,
    rel_pair,
    edge_left,
    edge_right,
    edge_slot,
    edge_weight,
):
    block_len = left_block.shape[0]
    left_half = left_block.astype(jnp.bfloat16)
    targets = edge_targets(edge_left, edge_right, edge_slot, edge_weight, block_len)
    grad_left = jnp.zeros(left_block.shape, jnp.float32)
    grad_right = jnp.zeros(right_half.shape, jnp.float32)
    rel_grads = []
    for slot_index in range(2):
        matrix = rel_pair[slot_index]
        projected = jnp.dot(left_half, matrix, preferred_element_type=jnp.float32).astype(
            jnp.bfloat16
        )
        scores = jnp.dot(projected, right_half.T, preferred_element_type=jnp.float32)
        score_grad = ((jax.nn.sigmoid(scores) - targets[slot_index]) / block_len).astype(
            jnp.bfloat16
        )
        carried = jnp.dot(score_grad, right_half, preferred_element_type=jnp.float32).astype(
            jnp.bfloat16
        )
        grad_left = grad_left + jnp.dot(carried, matrix.T, preferred_element_type=jnp.float32)
        grad_right = grad_right + jnp.dot(
            score_grad.T, projected, preferred_element_type=jnp.float32
        )
        rel_grads.append(jnp.dot(left_half.T, carried, preferred_element_type=jnp.float32))
    left_new, left_st_new = adagrad(left_block, left_st, grad_left)
    if right_block is None:
        return (left_new, left_st_new, None, (right_st, grad_right), rel_grads)
    right_new, right_st_new = adagrad(right_block, right_st, grad_right)
    return (left_new, left_st_new, right_new, right_st_new, rel_grads)


def partner_values(values, switch):
    count = lax.axis_size("bucket")

    def exchange(offset):
        pairs = [(b, b ^ offset) for b in range(count)]

        def run(*arrays):
            return tuple(lax.ppermute(array, "bucket", pairs) for array in arrays)

        return run

    branches = [exchange(offset) for offset in range(1, count)]
    return lax.switch(switch - 1, branches, *values)


def axis_bits(axis):
    count = lax.axis_size(axis)
    return [1 << j for j in range(count.bit_length() - 1)]


def halving_sum(chunks, axis, order, done=()):
    count = lax.axis_size(axis)
    index = lax.axis_index(axis)
    current = chunks
    done = list(done)
    for bit in order:
        lower = 1
        for other in axis_bits(axis):
            if other < bit and other not in done:
                lower *= 2
        upper = current.shape[0] // (2 * lower)
        split = current.reshape((upper, 2, lower) + current.shape[1:])
        mine = (index // bit) % 2
        keep = lax.dynamic_index_in_dim(split, mine, axis=1, keepdims=False)
        send = lax.dynamic_index_in_dim(split, 1 - mine, axis=1, keepdims=False)
        got = lax.ppermute(send, axis, [(k, k ^ bit) for k in range(count)])
        current = (keep + got).reshape((upper * lower,) + current.shape[1:])
        done.append(bit)
    return current[0]


def doubling_gather(piece, axis, order):
    count = lax.axis_size(axis)
    index = lax.axis_index(axis)
    current = piece[None]
    done = []
    for bit in order:
        lower = 1
        for other in done:
            if other < bit:
                lower *= 2
        upper = current.shape[0] // lower
        got = lax.ppermute(current, axis, [(k, k ^ bit) for k in range(count)])
        mine = (index // bit) % 2
        ours = current.reshape((upper, 1, lower) + piece.shape)
        theirs = got.reshape((upper, 1, lower) + piece.shape)
        joined = jnp.zeros((upper, 2, lower) + piece.shape, piece.dtype)
        joined = lax.dynamic_update_index_in_dim(joined, ours, mine, axis=1)
        joined = lax.dynamic_update_index_in_dim(joined, theirs, 1 - mine, axis=1)
        current = joined.reshape((upper * 2 * lower,) + piece.shape)
        done.append(bit)
    return current


def selected_term(gradients, rel_ids, devices, per_device, pieces, columns):
    width = gradients[0].shape[0]
    wanted = devices[:, None] * per_device + jnp.arange(per_device, dtype=jnp.int32)[None, :]
    total = jnp.zeros((devices.shape[0], per_device, width, columns.stop - columns.start), jnp.float32)
    for slot_index, gradient in enumerate(gradients):
        hit = (rel_ids[slot_index] == wanted)[:, :, None, None]
        total = total + jnp.where(hit, gradient[None, None, :, columns], jnp.float32(0.0))
    rows = per_device * width
    return total.reshape(devices.shape[0], pieces, rows // pieces, columns.stop - columns.start)


def split_bits(array, axis_names, bits_by_axis, order):
    lead = []
    shape = []
    for name in axis_names:
        bits = bits_by_axis[name]
        for bit in bits[::-1]:
            lead.append((name, bit))
            shape.append(2)
    array = array.reshape(tuple(shape) + array.shape[len(axis_names) :])
    perm = [lead.index(step) for step in order] + list(range(len(lead), array.ndim))
    return jnp.transpose(array, perm)


def halving_steps(current, order):
    for step_index, (name, bit) in enumerate(order):
        count = lax.axis_size(name)
        mine = (lax.axis_index(name) // bit) % 2
        keep = lax.dynamic_index_in_dim(current, mine, axis=0, keepdims=False)
        send = lax.dynamic_index_in_dim(current, 1 - mine, axis=0, keepdims=False)
        got = lax.ppermute(send, name, [(k, k ^ bit) for k in range(count)])
        current = keep + got
    return current


def doubling_steps(piece, name, order):
    count = lax.axis_size(name)
    current = piece
    dims = []
    for bit in order:
        got = lax.ppermute(current, name, [(k, k ^ bit) for k in range(count)])
        mine = (lax.axis_index(name) // bit) % 2
        current = jnp.where(mine == 0, jnp.stack([current, got]), jnp.stack([got, current]))
        dims = [bit] + dims
    natural = sorted(dims, reverse=True)
    current = jnp.transpose(current, [dims.index(bit) for bit in natural] + list(range(len(dims), current.ndim)))
    return current.reshape((-1,) + piece.shape[1:])


def reduce_gradients(gradients, rel_ids, rel_total, width, low, switch):
    rel_count = lax.axis_size("rel")
    bucket_count = lax.axis_size("bucket")
    per_device = rel_total // rel_count
    rel_bits = axis_bits("rel")
    bucket_bits = axis_bits("bucket")
    first = rel_bits[0]
    mine = (lax.axis_index("rel") // first) % 2
    owners = jnp.arange(rel_count, dtype=jnp.int32).reshape(-1, 2, first)
    kept = lax.dynamic_index_in_dim(owners, mine, axis=1, keepdims=False).reshape(-1)
    sent = lax.dynamic_index_in_dim(owners, 1 - mine, axis=1, keepdims=False).reshape(-1)
    rest = rel_bits[1:]
    bits_by_axis = {"rel": rest, "bucket": bucket_bits}
    rel_steps = [("rel", bit) for bit in rest]
    bucket_steps = [("bucket", bit) for bit in bucket_bits]
    streams = [
        (bucket_steps + rel_steps, bucket_bits[::-1]),
        (rel_steps + bucket_steps, bucket_bits[:1] + bucket_bits[1:][::-1]),
    ]
    band = width // len(streams)
    everything = slice(0, width)
    keep = selected_term(gradients, rel_ids, kept, per_device, bucket_count, everything)
    send = selected_term(gradients, rel_ids, sent, per_device, bucket_count, everything)
    full = keep + lax.ppermute(send, "rel", [(k, k ^ first) for k in range(rel_count)])
    keeps = []
    sends = []
    for stream_index, (order, _) in enumerate(streams):
        part = full[..., stream_index * band : (stream_index + 1) * band]
        current = split_bits(part, ("rel", "bucket"), bits_by_axis, order)
        name, bit = order[0]
        side = (lax.axis_index(name) // bit) % 2
        keeps.append(lax.dynamic_index_in_dim(current, side, axis=0, keepdims=False))
        sends.append(lax.dynamic_index_in_dim(current, 1 - side, axis=0, keepdims=False))
    count = lax.axis_size("bucket")

    def first_step(offset):
        pairs = [(b, b ^ offset) for b in range(count)]

        def run(low_part, *parts):
            moved = []
            for (order, _), part in zip(streams, parts):
                name, bit = order[0]
                size = lax.axis_size(name)
                moved.append(lax.ppermute(part, name, [(k, k ^ bit) for k in range(size)]))
            return (lax.ppermute(low_part, "bucket", pairs),) + tuple(moved)

        return run

    results = lax.switch(
        switch - 1, [first_step(offset) for offset in range(1, count)], low, *sends
    )
    block_low = results[0]
    pieces = []
    for (order, _), keep, got in zip(streams, keeps, results[1:]):
        pieces.append(halving_steps(keep + got, order[1:]))
    joined = jnp.concatenate(pieces, axis=1)
    return doubling_steps(joined, "bucket", streams[0][1]), block_low


def on_device(
    left_rows,
    left_state,
    right_rows,
    right_state,
    relations,
    fetch_ids,
    edge_left,
    edge_right,
    edge_slot,
    edge_weight,
    matching,
):
    width = relations.shape[1]
    rel_table = doubling_gather(relations, "rel", axis_bits("rel")[::-1]).reshape(
        -1, width, width
    )
    rel_total = rel_table.shape[0]
    rel_ids = fetch_ids[0, 0]
    switch = matching[0]
    table_left, state_left = (left_rows, left_state)
    row_block, state_block = (right_rows, right_state)
    gradients = []
    right_half = row_block.astype(jnp.bfloat16)
    for round_index in range(2):
        rel_pair = jnp.take(rel_table, rel_ids[2 * round_index : 2 * round_index + 2], axis=0)
        table_left, state_left, row_block, state_block, rel_grads = one_round(
            table_left,
            state_left,
            row_block,
            state_block,
            right_half,
            rel_pair,
            edge_left[0, 0, round_index],
            edge_right[0, 0, round_index],
            edge_slot[0, 0, round_index],
            edge_weight[0, 0, round_index],
        )
        gradients.extend(rel_grads)
        if round_index == 0:
            rounded = lax.reduce_precision(row_block, exponent_bits=8, mantissa_bits=7)
            high = rounded.astype(jnp.bfloat16)
            low = (row_block - rounded).astype(jnp.bfloat16)
            state_rounded = lax.reduce_precision(state_block, exponent_bits=8, mantissa_bits=7)
            state_pair = jnp.concatenate([state_rounded, state_block - state_rounded])
            block_len, row_width = high.shape
            state_rows = -(-state_pair.shape[0] // row_width)
            state_pair = jnp.pad(state_pair, (0, state_rows * row_width - state_pair.shape[0]))
            packed = jnp.concatenate(
                [high, state_pair.astype(jnp.bfloat16).reshape(state_rows, row_width)]
            )
            (their_packed,) = partner_values((packed,), switch)
            right_half = their_packed[:block_len]
            their_state = their_packed[block_len:].reshape(-1).astype(jnp.float32)
            state_block = their_state[:block_len] + their_state[block_len : 2 * block_len]
            block_high = right_half
            row_block = None

    right_st, grad_right = state_block
    owned, their_low = reduce_gradients(gradients, rel_ids, rel_total, width, low, switch)
    row_block, state_block = adagrad(
        block_high.astype(jnp.float32) + their_low.astype(jnp.float32), right_st, grad_right
    )
    return (table_left, state_left, row_block, state_block, owned.reshape(-1, width, width))


def solution(mesh):
    in_specs = (
        P(("bucket", "rel"), None),
        P(("bucket", "rel")),
        P(("bucket", "rel"), None),
        P(("bucket", "rel")),
        P("rel", None, None),
        P("bucket", "rel", None),
        P("bucket", "rel", None, None),
        P("bucket", "rel", None, None),
        P("bucket", "rel", None, None),
        P("bucket", "rel", None, None),
        P(),
    )
    out_specs = (
        P(("bucket", "rel"), None),
        P(("bucket", "rel")),
        P(("bucket", "rel"), None),
        P(("bucket", "rel")),
        P("rel", None, None),
    )
    return jax.shard_map(
        on_device, mesh=mesh, in_specs=in_specs, out_specs=out_specs, check_vma=False
    )
```

```python
import jax
import jax.numpy as jnp
from jax import lax
from jax.sharding import PartitionSpec as P

learn_rate = 0.1


def edge_targets(edge_left, edge_right, edge_slot, edge_weight, block_len):
    rows = jnp.arange(block_len, dtype=jnp.int32)
    weight = edge_weight.astype(jnp.float32)
    right_hot = (edge_right[:, None] == rows[None, :]).astype(jnp.bfloat16)
    left_hot = edge_left[:, None] == rows[None, :]
    targets = []
    for slot_index in range(2):
        scale = jnp.where(edge_slot == slot_index, weight, jnp.float32(0.0))
        left_w = jnp.where(left_hot, scale[:, None], jnp.float32(0.0)).astype(jnp.bfloat16)
        targets.append(
            lax.dot_general(
                left_w, right_hot, (((0,), (0,)), ((), ())), preferred_element_type=jnp.float32
            )
        )
    return targets


def adagrad(table, state, gradient):
    state_new = state + jnp.mean(gradient * gradient, axis=1)
    return (table - learn_rate * gradient / jnp.sqrt(state_new)[:, None], state_new)


def one_round(
    left_block,
    left_st,
    right_block,
    right_st,
    right_half,
    rel_pair,
    edge_left,
    edge_right,
    edge_slot,
    edge_weight,
):
    block_len = left_block.shape[0]
    left_half = left_block.astype(jnp.bfloat16)
    targets = edge_targets(edge_left, edge_right, edge_slot, edge_weight, block_len)
    grad_left = jnp.zeros(left_block.shape, jnp.float32)
    grad_right = jnp.zeros(right_half.shape, jnp.float32)
    rel_grads = []
    for slot_index in range(2):
        matrix = rel_pair[slot_index]
        projected = jnp.dot(left_half, matrix, preferred_element_type=jnp.float32).astype(
            jnp.bfloat16
        )
        scores = jnp.dot(projected, right_half.T, preferred_element_type=jnp.float32)
        score_grad = ((jax.nn.sigmoid(scores) - targets[slot_index]) / block_len).astype(
            jnp.bfloat16
        )
        carried = jnp.dot(score_grad, right_half, preferred_element_type=jnp.float32).astype(
            jnp.bfloat16
        )
        grad_left = grad_left + jnp.dot(carried, matrix.T, preferred_element_type=jnp.float32)
        grad_right = grad_right + jnp.dot(
            score_grad.T, projected, preferred_element_type=jnp.float32
        )
        rel_grads.append(jnp.dot(left_half.T, carried, preferred_element_type=jnp.float32))
    left_new, left_st_new = adagrad(left_block, left_st, grad_left)
    if right_block is None:
        return (left_new, left_st_new, None, (right_st, grad_right), rel_grads)
    right_new, right_st_new = adagrad(right_block, right_st, grad_right)
    return (left_new, left_st_new, right_new, right_st_new, rel_grads)


def partner_values(values, switch):
    count = lax.axis_size("bucket")

    def exchange(offset):
        pairs = [(b, b ^ offset) for b in range(count)]

        def run(*arrays):
            return tuple(lax.ppermute(array, "bucket", pairs) for array in arrays)

        return run

    branches = [exchange(offset) for offset in range(1, count)]
    return lax.switch(switch - 1, branches, *values)


def axis_bits(axis):
    count = lax.axis_size(axis)
    return [1 << j for j in range(count.bit_length() - 1)]


def halving_sum(chunks, axis, order, done=()):
    count = lax.axis_size(axis)
    index = lax.axis_index(axis)
    current = chunks
    done = list(done)
    for bit in order:
        lower = 1
        for other in axis_bits(axis):
            if other < bit and other not in done:
                lower *= 2
        upper = current.shape[0] // (2 * lower)
        split = current.reshape((upper, 2, lower) + current.shape[1:])
        mine = (index // bit) % 2
        keep = lax.dynamic_index_in_dim(split, mine, axis=1, keepdims=False)
        send = lax.dynamic_index_in_dim(split, 1 - mine, axis=1, keepdims=False)
        got = lax.ppermute(send, axis, [(k, k ^ bit) for k in range(count)])
        current = (keep + got).reshape((upper * lower,) + current.shape[1:])
        done.append(bit)
    return current[0]


def doubling_gather(piece, axis, order):
    count = lax.axis_size(axis)
    index = lax.axis_index(axis)
    current = piece[None]
    done = []
    for bit in order:
        lower = 1
        for other in done:
            if other < bit:
                lower *= 2
        upper = current.shape[0] // lower
        got = lax.ppermute(current, axis, [(k, k ^ bit) for k in range(count)])
        mine = (index // bit) % 2
        ours = current.reshape((upper, 1, lower) + piece.shape)
        theirs = got.reshape((upper, 1, lower) + piece.shape)
        joined = jnp.zeros((upper, 2, lower) + piece.shape, piece.dtype)
        joined = lax.dynamic_update_index_in_dim(joined, ours, mine, axis=1)
        joined = lax.dynamic_update_index_in_dim(joined, theirs, 1 - mine, axis=1)
        current = joined.reshape((upper * 2 * lower,) + piece.shape)
        done.append(bit)
    return current


def selected_term(gradients, rel_ids, devices, per_device, pieces, columns):
    width = gradients[0].shape[0]
    wanted = devices[:, None] * per_device + jnp.arange(per_device, dtype=jnp.int32)[None, :]
    total = jnp.zeros((devices.shape[0], per_device, width, columns.stop - columns.start), jnp.float32)
    for slot_index, gradient in enumerate(gradients):
        hit = (rel_ids[slot_index] == wanted)[:, :, None, None]
        total = total + jnp.where(hit, gradient[None, None, :, columns], jnp.float32(0.0))
    rows = per_device * width
    return total.reshape(devices.shape[0], pieces, rows // pieces, columns.stop - columns.start)


def split_bits(array, axis_names, bits_by_axis, order):
    lead = []
    shape = []
    for name in axis_names:
        bits = bits_by_axis[name]
        for bit in bits[::-1]:
            lead.append((name, bit))
            shape.append(2)
    array = array.reshape(tuple(shape) + array.shape[len(axis_names) :])
    perm = [lead.index(step) for step in order] + list(range(len(lead), array.ndim))
    return jnp.transpose(array, perm)


def halving_steps(current, order):
    for step_index, (name, bit) in enumerate(order):
        count = lax.axis_size(name)
        mine = (lax.axis_index(name) // bit) % 2
        keep = lax.dynamic_index_in_dim(current, mine, axis=0, keepdims=False)
        send = lax.dynamic_index_in_dim(current, 1 - mine, axis=0, keepdims=False)
        got = lax.ppermute(send, name, [(k, k ^ bit) for k in range(count)])
        current = keep + got
    return current


def doubling_steps(piece, name, order):
    count = lax.axis_size(name)
    current = piece
    dims = []
    for bit in order:
        got = lax.ppermute(current, name, [(k, k ^ bit) for k in range(count)])
        mine = (lax.axis_index(name) // bit) % 2
        current = jnp.where(mine == 0, jnp.stack([current, got]), jnp.stack([got, current]))
        dims = [bit] + dims
    natural = sorted(dims, reverse=True)
    current = jnp.transpose(current, [dims.index(bit) for bit in natural] + list(range(len(dims), current.ndim)))
    return current.reshape((-1,) + piece.shape[1:])


def reduce_gradients(gradients, rel_ids, rel_total, width, low, switch):
    rel_count = lax.axis_size("rel")
    bucket_count = lax.axis_size("bucket")
    per_device = rel_total // rel_count
    rel_bits = axis_bits("rel")
    bucket_bits = axis_bits("bucket")
    first = rel_bits[0]
    mine = (lax.axis_index("rel") // first) % 2
    owners = jnp.arange(rel_count, dtype=jnp.int32).reshape(-1, 2, first)
    kept = lax.dynamic_index_in_dim(owners, mine, axis=1, keepdims=False).reshape(-1)
    sent = lax.dynamic_index_in_dim(owners, 1 - mine, axis=1, keepdims=False).reshape(-1)
    rest = rel_bits[1:]
    bits_by_axis = {"rel": rest, "bucket": bucket_bits}
    rel_steps = [("rel", bit) for bit in rest]
    bucket_steps = [("bucket", bit) for bit in bucket_bits]
    streams = [
        (bucket_steps[:2] + rel_steps + bucket_steps[2:], bucket_bits[::-1]),
        (rel_steps + bucket_steps, bucket_bits[:1] + bucket_bits[1:][::-1]),
    ]
    band = width // len(streams)
    everything = slice(0, width)
    keep = selected_term(gradients, rel_ids, kept, per_device, bucket_count, everything)
    send = selected_term(gradients, rel_ids, sent, per_device, bucket_count, everything)
    full = keep + lax.ppermute(send, "rel", [(k, k ^ first) for k in range(rel_count)])
    keeps = []
    sends = []
    for stream_index, (order, _) in enumerate(streams):
        part = full[..., stream_index * band : (stream_index + 1) * band]
        current = split_bits(part, ("rel", "bucket"), bits_by_axis, order)
        name, bit = order[0]
        side = (lax.axis_index(name) // bit) % 2
        keeps.append(lax.dynamic_index_in_dim(current, side, axis=0, keepdims=False))
        sends.append(lax.dynamic_index_in_dim(current, 1 - side, axis=0, keepdims=False))
    count = lax.axis_size("bucket")

    def first_step(offset):
        pairs = [(b, b ^ offset) for b in range(count)]

        def run(low_part, *parts):
            moved = []
            for (order, _), part in zip(streams, parts):
                name, bit = order[0]
                size = lax.axis_size(name)
                moved.append(lax.ppermute(part, name, [(k, k ^ bit) for k in range(size)]))
            return (lax.ppermute(low_part, "bucket", pairs),) + tuple(moved)

        return run

    results = lax.switch(
        switch - 1, [first_step(offset) for offset in range(1, count)], low, *sends
    )
    block_low = results[0]
    outputs = []
    for (order, gather_order), keep, got in zip(streams, keeps, results[1:]):
        current = halving_steps(keep + got, order[1:])
        outputs.append(doubling_steps(current, "bucket", gather_order))
    return jnp.concatenate(outputs, axis=1), block_low


def on_device(
    left_rows,
    left_state,
    right_rows,
    right_state,
    relations,
    fetch_ids,
    edge_left,
    edge_right,
    edge_slot,
    edge_weight,
    matching,
):
    width = relations.shape[1]
    rel_table = doubling_gather(relations, "rel", axis_bits("rel")[::-1]).reshape(
        -1, width, width
    )
    rel_total = rel_table.shape[0]
    rel_ids = fetch_ids[0, 0]
    switch = matching[0]
    table_left, state_left = (left_rows, left_state)
    row_block, state_block = (right_rows, right_state)
    gradients = []
    right_half = row_block.astype(jnp.bfloat16)
    for round_index in range(2):
        rel_pair = jnp.take(rel_table, rel_ids[2 * round_index : 2 * round_index + 2], axis=0)
        table_left, state_left, row_block, state_block, rel_grads = one_round(
            table_left,
            state_left,
            row_block,
            state_block,
            right_half,
            rel_pair,
            edge_left[0, 0, round_index],
            edge_right[0, 0, round_index],
            edge_slot[0, 0, round_index],
            edge_weight[0, 0, round_index],
        )
        gradients.extend(rel_grads)
        if round_index == 0:
            rounded = lax.reduce_precision(row_block, exponent_bits=8, mantissa_bits=7)
            high = rounded.astype(jnp.bfloat16)
            low = (row_block - rounded).astype(jnp.bfloat16)
            state_rounded = lax.reduce_precision(state_block, exponent_bits=8, mantissa_bits=7)
            state_pair = jnp.concatenate([state_rounded, state_block - state_rounded])
            block_len, row_width = high.shape
            state_rows = -(-state_pair.shape[0] // row_width)
            state_pair = jnp.pad(state_pair, (0, state_rows * row_width - state_pair.shape[0]))
            packed = jnp.concatenate(
                [high, state_pair.astype(jnp.bfloat16).reshape(state_rows, row_width)]
            )
            (their_packed,) = partner_values((packed,), switch)
            right_half = their_packed[:block_len]
            their_state = their_packed[block_len:].reshape(-1).astype(jnp.float32)
            state_block = their_state[:block_len] + their_state[block_len : 2 * block_len]
            block_high = right_half
            row_block = None

    right_st, grad_right = state_block
    owned, their_low = reduce_gradients(gradients, rel_ids, rel_total, width, low, switch)
    row_block, state_block = adagrad(
        block_high.astype(jnp.float32) + their_low.astype(jnp.float32), right_st, grad_right
    )
    return (table_left, state_left, row_block, state_block, owned.reshape(-1, width, width))


def solution(mesh):
    in_specs = (
        P(("bucket", "rel"), None),
        P(("bucket", "rel")),
        P(("bucket", "rel"), None),
        P(("bucket", "rel")),
        P("rel", None, None),
        P("bucket", "rel", None),
        P("bucket", "rel", None, None),
        P("bucket", "rel", None, None),
        P("bucket", "rel", None, None),
        P("bucket", "rel", None, None),
        P(),
    )
    out_specs = (
        P(("bucket", "rel"), None),
        P(("bucket", "rel")),
        P(("bucket", "rel"), None),
        P(("bucket", "rel")),
        P("rel", None, None),
    )
    return jax.shard_map(
        on_device, mesh=mesh, in_specs=in_specs, out_specs=out_specs, check_vma=False
    )
```

```python
import jax
import jax.numpy as jnp
from jax import lax
from jax.sharding import PartitionSpec as P

learn_rate = 0.1


def edge_targets(edge_left, edge_right, edge_slot, edge_weight, block_len):
    rows = jnp.arange(block_len, dtype=jnp.int32)
    weight = edge_weight.astype(jnp.float32)
    right_hot = (edge_right[:, None] == rows[None, :]).astype(jnp.bfloat16)
    left_hot = edge_left[:, None] == rows[None, :]
    targets = []
    for slot_index in range(2):
        scale = jnp.where(edge_slot == slot_index, weight, jnp.float32(0.0))
        left_w = jnp.where(left_hot, scale[:, None], jnp.float32(0.0)).astype(jnp.bfloat16)
        targets.append(
            lax.dot_general(
                left_w, right_hot, (((0,), (0,)), ((), ())), preferred_element_type=jnp.float32
            )
        )
    return targets


def adagrad(table, state, gradient):
    state_new = state + jnp.mean(gradient * gradient, axis=1)
    return (table - learn_rate * gradient / jnp.sqrt(state_new)[:, None], state_new)


def one_round(
    left_block,
    left_st,
    right_block,
    right_st,
    right_half,
    rel_pair,
    edge_left,
    edge_right,
    edge_slot,
    edge_weight,
):
    block_len = left_block.shape[0]
    left_half = left_block.astype(jnp.bfloat16)
    targets = edge_targets(edge_left, edge_right, edge_slot, edge_weight, block_len)
    grad_left = jnp.zeros(left_block.shape, jnp.float32)
    grad_right = jnp.zeros(right_half.shape, jnp.float32)
    rel_grads = []
    for slot_index in range(2):
        matrix = rel_pair[slot_index]
        projected = jnp.dot(left_half, matrix, preferred_element_type=jnp.float32).astype(
            jnp.bfloat16
        )
        scores = jnp.dot(projected, right_half.T, preferred_element_type=jnp.float32)
        score_grad = ((jax.nn.sigmoid(scores) - targets[slot_index]) / block_len).astype(
            jnp.bfloat16
        )
        carried = jnp.dot(score_grad, right_half, preferred_element_type=jnp.float32).astype(
            jnp.bfloat16
        )
        grad_left = grad_left + jnp.dot(carried, matrix.T, preferred_element_type=jnp.float32)
        grad_right = grad_right + jnp.dot(
            score_grad.T, projected, preferred_element_type=jnp.float32
        )
        rel_grads.append(jnp.dot(left_half.T, carried, preferred_element_type=jnp.float32))
    left_new, left_st_new = adagrad(left_block, left_st, grad_left)
    if right_block is None:
        return (left_new, left_st_new, None, (right_st, grad_right), rel_grads)
    right_new, right_st_new = adagrad(right_block, right_st, grad_right)
    return (left_new, left_st_new, right_new, right_st_new, rel_grads)


def partner_values(values, switch):
    count = lax.axis_size("bucket")

    def exchange(offset):
        pairs = [(b, b ^ offset) for b in range(count)]

        def run(*arrays):
            return tuple(lax.ppermute(array, "bucket", pairs) for array in arrays)

        return run

    branches = [exchange(offset) for offset in range(1, count)]
    return lax.switch(switch - 1, branches, *values)


def axis_bits(axis):
    count = lax.axis_size(axis)
    return [1 << j for j in range(count.bit_length() - 1)]


def halving_sum(chunks, axis, order, done=()):
    count = lax.axis_size(axis)
    index = lax.axis_index(axis)
    current = chunks
    done = list(done)
    for bit in order:
        lower = 1
        for other in axis_bits(axis):
            if other < bit and other not in done:
                lower *= 2
        upper = current.shape[0] // (2 * lower)
        split = current.reshape((upper, 2, lower) + current.shape[1:])
        mine = (index // bit) % 2
        keep = lax.dynamic_index_in_dim(split, mine, axis=1, keepdims=False)
        send = lax.dynamic_index_in_dim(split, 1 - mine, axis=1, keepdims=False)
        got = lax.ppermute(send, axis, [(k, k ^ bit) for k in range(count)])
        current = (keep + got).reshape((upper * lower,) + current.shape[1:])
        done.append(bit)
    return current[0]


def doubling_gather(piece, axis, order):
    count = lax.axis_size(axis)
    index = lax.axis_index(axis)
    current = piece[None]
    done = []
    for bit in order:
        lower = 1
        for other in done:
            if other < bit:
                lower *= 2
        upper = current.shape[0] // lower
        got = lax.ppermute(current, axis, [(k, k ^ bit) for k in range(count)])
        mine = (index // bit) % 2
        ours = current.reshape((upper, 1, lower) + piece.shape)
        theirs = got.reshape((upper, 1, lower) + piece.shape)
        joined = jnp.zeros((upper, 2, lower) + piece.shape, piece.dtype)
        joined = lax.dynamic_update_index_in_dim(joined, ours, mine, axis=1)
        joined = lax.dynamic_update_index_in_dim(joined, theirs, 1 - mine, axis=1)
        current = joined.reshape((upper * 2 * lower,) + piece.shape)
        done.append(bit)
    return current


def selected_term(gradients, rel_ids, devices, per_device, pieces, columns):
    width = gradients[0].shape[0]
    wanted = devices[:, None] * per_device + jnp.arange(per_device, dtype=jnp.int32)[None, :]
    total = jnp.zeros((devices.shape[0], per_device, width, columns.stop - columns.start), jnp.float32)
    for slot_index, gradient in enumerate(gradients):
        hit = (rel_ids[slot_index] == wanted)[:, :, None, None]
        total = total + jnp.where(hit, gradient[None, None, :, columns], jnp.float32(0.0))
    rows = per_device * width
    return total.reshape(devices.shape[0], pieces, rows // pieces, columns.stop - columns.start)


def split_bits(array, axis_names, bits_by_axis, order):
    lead = []
    shape = []
    for name in axis_names:
        bits = bits_by_axis[name]
        for bit in bits[::-1]:
            lead.append((name, bit))
            shape.append(2)
    array = array.reshape(tuple(shape) + array.shape[len(axis_names) :])
    perm = [lead.index(step) for step in order] + list(range(len(lead), array.ndim))
    return jnp.transpose(array, perm)


def halving_steps(current, order):
    for step_index, (name, bit) in enumerate(order):
        count = lax.axis_size(name)
        mine = (lax.axis_index(name) // bit) % 2
        keep = lax.dynamic_index_in_dim(current, mine, axis=0, keepdims=False)
        send = lax.dynamic_index_in_dim(current, 1 - mine, axis=0, keepdims=False)
        got = lax.ppermute(send, name, [(k, k ^ bit) for k in range(count)])
        current = keep + got
    return current


def doubling_steps(piece, name, order):
    count = lax.axis_size(name)
    current = piece
    dims = []
    for bit in order:
        got = lax.ppermute(current, name, [(k, k ^ bit) for k in range(count)])
        mine = (lax.axis_index(name) // bit) % 2
        current = jnp.where(mine == 0, jnp.stack([current, got]), jnp.stack([got, current]))
        dims = [bit] + dims
    natural = sorted(dims, reverse=True)
    current = jnp.transpose(current, [dims.index(bit) for bit in natural] + list(range(len(dims), current.ndim)))
    return current.reshape((-1,) + piece.shape[1:])


def reduce_gradients(gradients, rel_ids, rel_total, width, low, switch):
    rel_count = lax.axis_size("rel")
    bucket_count = lax.axis_size("bucket")
    per_device = rel_total // rel_count
    rel_bits = axis_bits("rel")
    bucket_bits = axis_bits("bucket")
    first = rel_bits[0]
    mine = (lax.axis_index("rel") // first) % 2
    owners = jnp.arange(rel_count, dtype=jnp.int32).reshape(-1, 2, first)
    kept = lax.dynamic_index_in_dim(owners, mine, axis=1, keepdims=False).reshape(-1)
    sent = lax.dynamic_index_in_dim(owners, 1 - mine, axis=1, keepdims=False).reshape(-1)
    rest = rel_bits[1:]
    bits_by_axis = {"rel": rest, "bucket": bucket_bits}
    rel_steps = [("rel", bit) for bit in rest]
    bucket_steps = [("bucket", bit) for bit in bucket_bits]
    streams = [
        (bucket_steps[:2] + rel_steps + bucket_steps[2:], bucket_bits[::-1]),
        (rel_steps + bucket_steps, bucket_bits[2:][::-1] + bucket_bits[:2]),
    ]
    band = width // len(streams)
    everything = slice(0, width)
    keep = selected_term(gradients, rel_ids, kept, per_device, bucket_count, everything)
    send = selected_term(gradients, rel_ids, sent, per_device, bucket_count, everything)
    full = keep + lax.ppermute(send, "rel", [(k, k ^ first) for k in range(rel_count)])
    keeps = []
    sends = []
    for stream_index, (order, _) in enumerate(streams):
        part = full[..., stream_index * band : (stream_index + 1) * band]
        current = split_bits(part, ("rel", "bucket"), bits_by_axis, order)
        name, bit = order[0]
        side = (lax.axis_index(name) // bit) % 2
        keeps.append(lax.dynamic_index_in_dim(current, side, axis=0, keepdims=False))
        sends.append(lax.dynamic_index_in_dim(current, 1 - side, axis=0, keepdims=False))
    count = lax.axis_size("bucket")

    def first_step(offset):
        pairs = [(b, b ^ offset) for b in range(count)]

        def run(low_part, *parts):
            moved = []
            for (order, _), part in zip(streams, parts):
                name, bit = order[0]
                size = lax.axis_size(name)
                moved.append(lax.ppermute(part, name, [(k, k ^ bit) for k in range(size)]))
            return (lax.ppermute(low_part, "bucket", pairs),) + tuple(moved)

        return run

    results = lax.switch(
        switch - 1, [first_step(offset) for offset in range(1, count)], low, *sends
    )
    block_low = results[0]
    outputs = []
    for (order, gather_order), keep, got in zip(streams, keeps, results[1:]):
        current = halving_steps(keep + got, order[1:])
        outputs.append(doubling_steps(current, "bucket", gather_order))
    return jnp.concatenate(outputs, axis=1), block_low


def on_device(
    left_rows,
    left_state,
    right_rows,
    right_state,
    relations,
    fetch_ids,
    edge_left,
    edge_right,
    edge_slot,
    edge_weight,
    matching,
):
    width = relations.shape[1]
    rel_table = doubling_gather(relations, "rel", axis_bits("rel")[::-1]).reshape(
        -1, width, width
    )
    rel_total = rel_table.shape[0]
    rel_ids = fetch_ids[0, 0]
    switch = matching[0]
    table_left, state_left = (left_rows, left_state)
    row_block, state_block = (right_rows, right_state)
    gradients = []
    right_half = row_block.astype(jnp.bfloat16)
    for round_index in range(2):
        rel_pair = jnp.take(rel_table, rel_ids[2 * round_index : 2 * round_index + 2], axis=0)
        table_left, state_left, row_block, state_block, rel_grads = one_round(
            table_left,
            state_left,
            row_block,
            state_block,
            right_half,
            rel_pair,
            edge_left[0, 0, round_index],
            edge_right[0, 0, round_index],
            edge_slot[0, 0, round_index],
            edge_weight[0, 0, round_index],
        )
        gradients.extend(rel_grads)
        if round_index == 0:
            rounded = lax.reduce_precision(row_block, exponent_bits=8, mantissa_bits=7)
            high = rounded.astype(jnp.bfloat16)
            low = (row_block - rounded).astype(jnp.bfloat16)
            state_rounded = lax.reduce_precision(state_block, exponent_bits=8, mantissa_bits=7)
            state_pair = jnp.concatenate([state_rounded, state_block - state_rounded])
            block_len, row_width = high.shape
            state_rows = -(-state_pair.shape[0] // row_width)
            state_pair = jnp.pad(state_pair, (0, state_rows * row_width - state_pair.shape[0]))
            packed = jnp.concatenate(
                [high, state_pair.astype(jnp.bfloat16).reshape(state_rows, row_width)]
            )
            (their_packed,) = partner_values((packed,), switch)
            right_half = their_packed[:block_len]
            their_state = their_packed[block_len:].reshape(-1).astype(jnp.float32)
            state_block = their_state[:block_len] + their_state[block_len : 2 * block_len]
            block_high = right_half
            row_block = None

    right_st, grad_right = state_block
    owned, their_low = reduce_gradients(gradients, rel_ids, rel_total, width, low, switch)
    row_block, state_block = adagrad(
        block_high.astype(jnp.float32) + their_low.astype(jnp.float32), right_st, grad_right
    )
    return (table_left, state_left, row_block, state_block, owned.reshape(-1, width, width))


def solution(mesh):
    in_specs = (
        P(("bucket", "rel"), None),
        P(("bucket", "rel")),
        P(("bucket", "rel"), None),
        P(("bucket", "rel")),
        P("rel", None, None),
        P("bucket", "rel", None),
        P("bucket", "rel", None, None),
        P("bucket", "rel", None, None),
        P("bucket", "rel", None, None),
        P("bucket", "rel", None, None),
        P(),
    )
    out_specs = (
        P(("bucket", "rel"), None),
        P(("bucket", "rel")),
        P(("bucket", "rel"), None),
        P(("bucket", "rel")),
        P("rel", None, None),
    )
    return jax.shard_map(
        on_device, mesh=mesh, in_specs=in_specs, out_specs=out_specs, check_vma=False
    )
```

```python
import jax
import jax.numpy as jnp
from jax import lax
from jax.sharding import PartitionSpec as P

learn_rate = 0.1


def edge_targets(edge_left, edge_right, edge_slot, edge_weight, block_len):
    rows = jnp.arange(block_len, dtype=jnp.int32)
    weight = edge_weight.astype(jnp.float32)
    right_hot = (edge_right[:, None] == rows[None, :]).astype(jnp.bfloat16)
    left_hot = edge_left[:, None] == rows[None, :]
    targets = []
    for slot_index in range(2):
        scale = jnp.where(edge_slot == slot_index, weight, jnp.float32(0.0))
        left_w = jnp.where(left_hot, scale[:, None], jnp.float32(0.0)).astype(jnp.bfloat16)
        targets.append(
            lax.dot_general(
                left_w, right_hot, (((0,), (0,)), ((), ())), preferred_element_type=jnp.float32
            )
        )
    return targets


def adagrad(table, state, gradient):
    state_new = state + jnp.mean(gradient * gradient, axis=1)
    return (table - learn_rate * gradient / jnp.sqrt(state_new)[:, None], state_new)


def one_round(
    left_block,
    left_st,
    right_block,
    right_st,
    right_half,
    rel_pair,
    edge_left,
    edge_right,
    edge_slot,
    edge_weight,
):
    block_len = left_block.shape[0]
    left_half = left_block.astype(jnp.bfloat16)
    targets = edge_targets(edge_left, edge_right, edge_slot, edge_weight, block_len)
    grad_left = jnp.zeros(left_block.shape, jnp.float32)
    grad_right = jnp.zeros(right_half.shape, jnp.float32)
    rel_grads = []
    for slot_index in range(2):
        matrix = rel_pair[slot_index]
        projected = jnp.dot(left_half, matrix, preferred_element_type=jnp.float32).astype(
            jnp.bfloat16
        )
        scores = jnp.dot(projected, right_half.T, preferred_element_type=jnp.float32)
        score_grad = ((jax.nn.sigmoid(scores) - targets[slot_index]) / block_len).astype(
            jnp.bfloat16
        )
        carried = jnp.dot(score_grad, right_half, preferred_element_type=jnp.float32).astype(
            jnp.bfloat16
        )
        grad_left = grad_left + jnp.dot(carried, matrix.T, preferred_element_type=jnp.float32)
        grad_right = grad_right + jnp.dot(
            score_grad.T, projected, preferred_element_type=jnp.float32
        )
        rel_grads.append(jnp.dot(left_half.T, carried, preferred_element_type=jnp.float32))
    left_new, left_st_new = adagrad(left_block, left_st, grad_left)
    if right_block is None:
        return (left_new, left_st_new, None, (right_st, grad_right), rel_grads)
    right_new, right_st_new = adagrad(right_block, right_st, grad_right)
    return (left_new, left_st_new, right_new, right_st_new, rel_grads)


def partner_values(values, switch):
    count = lax.axis_size("bucket")

    def exchange(offset):
        pairs = [(b, b ^ offset) for b in range(count)]

        def run(*arrays):
            return tuple(lax.ppermute(array, "bucket", pairs) for array in arrays)

        return run

    branches = [exchange(offset) for offset in range(1, count)]
    return lax.switch(switch - 1, branches, *values)


def axis_bits(axis):
    count = lax.axis_size(axis)
    return [1 << j for j in range(count.bit_length() - 1)]


def halving_sum(chunks, axis, order, done=()):
    count = lax.axis_size(axis)
    index = lax.axis_index(axis)
    current = chunks
    done = list(done)
    for bit in order:
        lower = 1
        for other in axis_bits(axis):
            if other < bit and other not in done:
                lower *= 2
        upper = current.shape[0] // (2 * lower)
        split = current.reshape((upper, 2, lower) + current.shape[1:])
        mine = (index // bit) % 2
        keep = lax.dynamic_index_in_dim(split, mine, axis=1, keepdims=False)
        send = lax.dynamic_index_in_dim(split, 1 - mine, axis=1, keepdims=False)
        got = lax.ppermute(send, axis, [(k, k ^ bit) for k in range(count)])
        current = (keep + got).reshape((upper * lower,) + current.shape[1:])
        done.append(bit)
    return current[0]


def doubling_gather(piece, axis, order):
    count = lax.axis_size(axis)
    index = lax.axis_index(axis)
    current = piece[None]
    done = []
    for bit in order:
        lower = 1
        for other in done:
            if other < bit:
                lower *= 2
        upper = current.shape[0] // lower
        got = lax.ppermute(current, axis, [(k, k ^ bit) for k in range(count)])
        mine = (index // bit) % 2
        ours = current.reshape((upper, 1, lower) + piece.shape)
        theirs = got.reshape((upper, 1, lower) + piece.shape)
        joined = jnp.zeros((upper, 2, lower) + piece.shape, piece.dtype)
        joined = lax.dynamic_update_index_in_dim(joined, ours, mine, axis=1)
        joined = lax.dynamic_update_index_in_dim(joined, theirs, 1 - mine, axis=1)
        current = joined.reshape((upper * 2 * lower,) + piece.shape)
        done.append(bit)
    return current


def selected_term(gradients, rel_ids, devices, per_device, pieces, columns):
    width = gradients[0].shape[0]
    wanted = devices[:, None] * per_device + jnp.arange(per_device, dtype=jnp.int32)[None, :]
    total = jnp.zeros((devices.shape[0], per_device, width, columns.stop - columns.start), jnp.float32)
    for slot_index, gradient in enumerate(gradients):
        hit = (rel_ids[slot_index] == wanted)[:, :, None, None]
        total = total + jnp.where(hit, gradient[None, None, :, columns], jnp.float32(0.0))
    rows = per_device * width
    return total.reshape(devices.shape[0], pieces, rows // pieces, columns.stop - columns.start)


def split_bits(array, axis_names, bits_by_axis, order):
    lead = []
    shape = []
    for name in axis_names:
        bits = bits_by_axis[name]
        for bit in bits[::-1]:
            lead.append((name, bit))
            shape.append(2)
    array = array.reshape(tuple(shape) + array.shape[len(axis_names) :])
    perm = [lead.index(step) for step in order] + list(range(len(lead), array.ndim))
    return jnp.transpose(array, perm)


def halving_steps(current, order):
    for step_index, (name, bit) in enumerate(order):
        count = lax.axis_size(name)
        mine = (lax.axis_index(name) // bit) % 2
        keep = lax.dynamic_index_in_dim(current, mine, axis=0, keepdims=False)
        send = lax.dynamic_index_in_dim(current, 1 - mine, axis=0, keepdims=False)
        got = lax.ppermute(send, name, [(k, k ^ bit) for k in range(count)])
        current = keep + got
    return current


def doubling_steps(piece, name, order):
    count = lax.axis_size(name)
    current = piece
    dims = []
    for bit in order:
        got = lax.ppermute(current, name, [(k, k ^ bit) for k in range(count)])
        mine = (lax.axis_index(name) // bit) % 2
        current = jnp.where(mine == 0, jnp.stack([current, got]), jnp.stack([got, current]))
        dims = [bit] + dims
    natural = sorted(dims, reverse=True)
    current = jnp.transpose(current, [dims.index(bit) for bit in natural] + list(range(len(dims), current.ndim)))
    return current.reshape((-1,) + piece.shape[1:])


def reduce_gradients(gradients, rel_ids, rel_total, width, low, switch):
    rel_count = lax.axis_size("rel")
    bucket_count = lax.axis_size("bucket")
    per_device = rel_total // rel_count
    rel_bits = axis_bits("rel")
    bucket_bits = axis_bits("bucket")
    first = rel_bits[0]
    mine = (lax.axis_index("rel") // first) % 2
    owners = jnp.arange(rel_count, dtype=jnp.int32).reshape(-1, 2, first)
    kept = lax.dynamic_index_in_dim(owners, mine, axis=1, keepdims=False).reshape(-1)
    sent = lax.dynamic_index_in_dim(owners, 1 - mine, axis=1, keepdims=False).reshape(-1)
    rest = rel_bits[1:]
    bits_by_axis = {"rel": rest, "bucket": bucket_bits}
    rel_steps = [("rel", bit) for bit in rest]
    bucket_steps = [("bucket", bit) for bit in bucket_bits]
    streams = [
        (bucket_steps[:1] + rel_steps + bucket_steps[1:], bucket_bits[::-1]),
        (rel_steps + bucket_steps, bucket_bits[:1] + bucket_bits[1:][::-1]),
    ]
    band = width // len(streams)
    everything = slice(0, width)
    keep = selected_term(gradients, rel_ids, kept, per_device, bucket_count, everything)
    send = selected_term(gradients, rel_ids, sent, per_device, bucket_count, everything)
    full = keep + lax.ppermute(send, "rel", [(k, k ^ first) for k in range(rel_count)])
    keeps = []
    sends = []
    for stream_index, (order, _) in enumerate(streams):
        part = full[..., stream_index * band : (stream_index + 1) * band]
        current = split_bits(part, ("rel", "bucket"), bits_by_axis, order)
        name, bit = order[0]
        side = (lax.axis_index(name) // bit) % 2
        keeps.append(lax.dynamic_index_in_dim(current, side, axis=0, keepdims=False))
        sends.append(lax.dynamic_index_in_dim(current, 1 - side, axis=0, keepdims=False))
    count = lax.axis_size("bucket")

    def first_step(offset):
        pairs = [(b, b ^ offset) for b in range(count)]

        def run(low_part, *parts):
            moved = []
            for (order, _), part in zip(streams, parts):
                name, bit = order[0]
                size = lax.axis_size(name)
                moved.append(lax.ppermute(part, name, [(k, k ^ bit) for k in range(size)]))
            return (lax.ppermute(low_part, "bucket", pairs),) + tuple(moved)

        return run

    results = lax.switch(
        switch - 1, [first_step(offset) for offset in range(1, count)], low, *sends
    )
    block_low = results[0]
    outputs = []
    for (order, gather_order), keep, got in zip(streams, keeps, results[1:]):
        current = halving_steps(keep + got, order[1:])
        outputs.append(doubling_steps(current, "bucket", gather_order))
    return jnp.concatenate(outputs, axis=1), block_low


def on_device(
    left_rows,
    left_state,
    right_rows,
    right_state,
    relations,
    fetch_ids,
    edge_left,
    edge_right,
    edge_slot,
    edge_weight,
    matching,
):
    width = relations.shape[1]
    rel_table = doubling_gather(relations, "rel", axis_bits("rel")[::-1]).reshape(
        -1, width, width
    )
    rel_total = rel_table.shape[0]
    rel_ids = fetch_ids[0, 0]
    switch = matching[0]
    table_left, state_left = (left_rows, left_state)
    row_block, state_block = (right_rows, right_state)
    gradients = []
    right_half = row_block.astype(jnp.bfloat16)
    for round_index in range(2):
        rel_pair = jnp.take(rel_table, rel_ids[2 * round_index : 2 * round_index + 2], axis=0)
        table_left, state_left, row_block, state_block, rel_grads = one_round(
            table_left,
            state_left,
            row_block,
            state_block,
            right_half,
            rel_pair,
            edge_left[0, 0, round_index],
            edge_right[0, 0, round_index],
            edge_slot[0, 0, round_index],
            edge_weight[0, 0, round_index],
        )
        gradients.extend(rel_grads)
        if round_index == 0:
            rounded = lax.reduce_precision(row_block, exponent_bits=8, mantissa_bits=7)
            high = rounded.astype(jnp.bfloat16)
            low = (row_block - rounded).astype(jnp.bfloat16)
            state_rounded = lax.reduce_precision(state_block, exponent_bits=8, mantissa_bits=7)
            state_pair = jnp.concatenate([state_rounded, state_block - state_rounded])
            block_len, row_width = high.shape
            state_rows = -(-state_pair.shape[0] // row_width)
            state_pair = jnp.pad(state_pair, (0, state_rows * row_width - state_pair.shape[0]))
            packed = jnp.concatenate(
                [high, state_pair.astype(jnp.bfloat16).reshape(state_rows, row_width)]
            )
            (their_packed,) = partner_values((packed,), switch)
            right_half = their_packed[:block_len]
            their_state = their_packed[block_len:].reshape(-1).astype(jnp.float32)
            state_block = their_state[:block_len] + their_state[block_len : 2 * block_len]
            block_high = right_half
            row_block = None

    right_st, grad_right = state_block
    owned, their_low = reduce_gradients(gradients, rel_ids, rel_total, width, low, switch)
    row_block, state_block = adagrad(
        block_high.astype(jnp.float32) + their_low.astype(jnp.float32), right_st, grad_right
    )
    return (table_left, state_left, row_block, state_block, owned.reshape(-1, width, width))


def solution(mesh):
    in_specs = (
        P(("bucket", "rel"), None),
        P(("bucket", "rel")),
        P(("bucket", "rel"), None),
        P(("bucket", "rel")),
        P("rel", None, None),
        P("bucket", "rel", None),
        P("bucket", "rel", None, None),
        P("bucket", "rel", None, None),
        P("bucket", "rel", None, None),
        P("bucket", "rel", None, None),
        P(),
    )
    out_specs = (
        P(("bucket", "rel"), None),
        P(("bucket", "rel")),
        P(("bucket", "rel"), None),
        P(("bucket", "rel")),
        P("rel", None, None),
    )
    return jax.shard_map(
        on_device, mesh=mesh, in_specs=in_specs, out_specs=out_specs, check_vma=False
    )
```
